256 devices in a mesh: dp: 32 (over y, z), tensor: 8 (over x, core).
Axes of the slice: x: 4, y: 4, z: 8, core: 2. Of those that a mesh axis runs over, the one named last changes fastest.
Arguments:
- residual_in: bfloat16 [2048, 2048], P(('dp', 'tensor')), may hold values from -6 to 6
- attn_gain: float32 [2048], replicated, may hold values from 0.5 to 1.5
- query_weight: bfloat16 [2048, 4096], P(None, 'tensor'), may hold values from -0.125 to 0.125
- kv_weight: bfloat16 [2048, 1024], P(None, 'tensor'), may hold values from -0.125 to 0.125
- query_gain: float32 [128], replicated, may hold values from 0.25 to 1.75
- key_gain: float32 [128], replicated, may hold values from 0.25 to 1.75
- out_weight: bfloat16 [4096, 2048], P('tensor'), may hold values from -0.09375 to 0.09375
- moe_gain: float32 [2048], replicated, may hold values from 0.5 to 1.5
- gate_weight: bfloat16 [128, 2048, 768], P('dp', None, 'tensor'), may hold values from -0.1875 to 0.1875
- lift_weight: bfloat16 [128, 2048, 768], P('dp', None, 'tensor'), may hold values from -0.1875 to 0.1875
- down_weight: bfloat16 [128, 768, 2048], P('dp', 'tensor'), may hold values from -0.21875 to 0.21875
- routes: int32 [2048, 8], P('dp'), may hold values from 0 to 127, as said below
- route_weights: float32 [2048, 8], P('dp'), may hold values from 0.5 to 1
- prefix_cache: bfloat16 [64, 2048, 1024], P('dp', 'tensor'), may hold values from -250 to 250
- suffix_cache: bfloat16 [2048, 128, 1024], P('dp', 'tensor'), may hold values from -250 to 250
- prefix_len: int32 [64], P('dp'), may hold values from 1 to 2048, as said below
- suffix_len: int32 [2048], P('dp'), may hold values from 1 to 128, as said below
- request_group: int32 [2048], P('dp'), may hold values from 0 to 63, as said below
Outputs:
- layer_out: bfloat16 [2048, 2048], P(('dp', 'tensor'))
- new_cache_rows: bfloat16 [2048, 1024], P('dp', 'tensor')
The draws below stay inside these ranges and needn't reach their ends.
Inputs may be any that keep to these rules, and one draw needn't show every extreme that they name: `routes`: each block of 64 rows (the requests of one index of dp) names 64 of the experts exactly 8 times each and no other expert; one expert is among them in every block. `request_group`: request r belongs to one of the groups (r // 64) * 2 to (r // 64) * 2 + 1. `prefix_len`: some shared prompt has all 2048 slots live. `suffix_len`: some request has all 128 suffix slots live.
All inputs are finite; a program needn't handle non-finite values.
Results may differ from the reference program's by a relative error of at most 0.02.
Values may be sent and summed in bfloat16 or wider, within the bound.
No kernel may reach another device: no remote copies, remote signals or barrier semaphores. Data moves between devices by JAX's collectives and lax.ppermute only.
A program may use at most 128 MiB of HBM per device.

```python
import math
import jax
import jax.numpy as jnp
from jax import lax

D = 2048
HEADS = 32
KVH = 4
HD = 128
FF_E = 768
TOPK = 8
REQ_DEV = 64
GRP_DEV = 2
PRE = 2048
SUF = 128
TOKENS = 2048
GROUPS = 64
EXPERTS = 128
CAP = 8
N_DP = 32


def cache_values(key, count_rows, length):
    width = 2 * KVH * HD
    values = jnp.clip(jax.random.normal(jax.random.fold_in(key, 11), (count_rows, length, width), jnp.float32), -6.0, 6.0)
    return values.astype(jnp.bfloat16)


def draw_prefix_cache(key, part):
    return cache_values(key, GROUPS, PRE)


def draw_suffix_cache(key, part):
    return cache_values(key, TOKENS, SUF)


def bounded_lengths(key, count_rows, longest):
    lengths = jax.random.randint(jax.random.fold_in(key, 21), (count_rows,), 1, longest + 1)
    chosen = jax.random.randint(jax.random.fold_in(key, 22), (), 0, count_rows)
    return jnp.where(jnp.arange(count_rows) == chosen, longest, lengths).astype(jnp.int32)


def draw_prefix_len(key, part):
    return bounded_lengths(key, GROUPS, PRE)


def draw_suffix_len(key, part):
    return bounded_lengths(key, TOKENS, SUF)


def draw_request_group(key, part):
    local_group = jax.random.randint(jax.random.fold_in(key, 31), (TOKENS,), 0, GRP_DEV)
    return (jnp.arange(TOKENS) // REQ_DEV * GRP_DEV + local_group).astype(jnp.int32)


def row_order(order_key):
    return jax.random.permutation(order_key, REQ_DEV)


def choice_order(order_key):
    return jax.random.permutation(order_key, TOPK)


def draw_routes(key, part):
    loaded = EXPERTS // 2
    stride = loaded // TOPK
    blocks = TOKENS // REQ_DEV
    common = jax.random.randint(jax.random.fold_in(key, 41), (), 0, EXPERTS).astype(jnp.int32)

    def one_block(index):
        block_key = jax.random.fold_in(jax.random.fold_in(key, 42), index)
        others = jax.random.permutation(jax.random.fold_in(block_key, 1), EXPERTS - 1).astype(jnp.int32)
        others = jnp.where(others >= common, others + 1, others)
        chosen = jnp.concatenate([common[None], others[:loaded - 1]])
        chosen = jax.random.permutation(jax.random.fold_in(block_key, 2), chosen)
        column_keys = jax.random.split(jax.random.fold_in(block_key, 3), TOPK)
        orders = jax.vmap(row_order)(column_keys).astype(jnp.int32)
        position = TOPK * (orders.T % stride) + jnp.arange(TOPK).astype(jnp.int32)[None, :]
        named = chosen[position]
        shuffle_keys = jax.random.split(jax.random.fold_in(block_key, 4), REQ_DEV)
        shuffle = jax.vmap(choice_order)(shuffle_keys).astype(jnp.int32)
        return jnp.take_along_axis(named, shuffle, axis=1)
    return jax.vmap(one_block)(jnp.arange(blocks)).reshape(TOKENS, TOPK).astype(jnp.int32)


def block_levels(key, extent, shards, low, top_value):
    factor_of = 1.0
    for dim, parts in shards:
        heights = jax.random.uniform(jax.random.fold_in(jax.random.fold_in(key, 6), dim), (parts,), jnp.float32, low / len(shards), top_value / len(shards))
        factor_of = factor_of * jnp.repeat(jnp.exp(heights), extent[dim] // parts).reshape((-1,) + (1,) * (len(extent) - 1 - dim))
    return factor_of


def scatter_about(key, dims, scale, reach, pieces=(), held_as=jnp.bfloat16):
    entries = jax.random.normal(key, dims, jnp.float32) * scale
    if len(pieces) > 0:
        entries = block_levels(key, dims, pieces, -0.22, 0.18) * entries
    return jnp.clip(entries, min=-reach, max=reach).astype(held_as)


def setup_inputs(seed: int = 0) -> dict:
    streams_of = jax.random.split(jax.random.key(seed), 19)
    return {
        "residual_in": scatter_about(streams_of[0], (TOKENS, D), 1.0, 6.0, ((0, 256),)),
        "attn_gain": jnp.clip(1.0 + 0.1 * jax.random.normal(streams_of[1], (D,), jnp.float32), 0.5, 1.5),
        "query_weight": scatter_about(streams_of[2], (D, HEADS * HD), D ** -0.5, 0.125, ((1, 8),)),
        "kv_weight": scatter_about(streams_of[3], (D, 2 * KVH * HD), D ** -0.5, 0.125, ((1, 8),)),
        "query_gain": jnp.clip(1.0 + 0.15 * jax.random.normal(streams_of[4], (HD,), jnp.float32), 0.25, 1.75),
        "key_gain": jnp.clip(1.0 + 0.15 * jax.random.normal(streams_of[5], (HD,), jnp.float32), 0.25, 1.75),
        "out_weight": scatter_about(streams_of[6], (HEADS * HD, D), (HEADS * HD) ** -0.5, 0.09375, ((0, 8),)),
        "moe_gain": jnp.clip(1.0 + 0.1 * jax.random.normal(streams_of[7], (D,), jnp.float32), 0.5, 1.5),
        "gate_weight": scatter_about(streams_of[8], (EXPERTS, D, FF_E), (D // 2) ** -0.5, 0.1875, ((0, 32), (2, 8))),
        "lift_weight": scatter_about(streams_of[9], (EXPERTS, D, FF_E), (D // 2) ** -0.5, 0.1875, ((0, 32), (2, 8))),
        "down_weight": scatter_about(streams_of[10], (EXPERTS, FF_E, D), FF_E ** -0.5, 0.21875, ((0, 32), (1, 8))),
        "routes": draw_routes(jax.random.fold_in(streams_of[18], 71), 0),
        "route_weights": jnp.clip(jnp.exp(math.log(1.0) - 0.6931472 * jax.random.uniform(streams_of[12], (TOKENS, TOPK), jnp.float32) ** block_levels(streams_of[12], (TOKENS, TOPK), ((0, 32),), -0.2, 0.2)), 0.5, 1.0),
        "prefix_cache": draw_prefix_cache(jax.random.fold_in(streams_of[18], 71), 0),
        "suffix_cache": draw_suffix_cache(jax.random.fold_in(streams_of[18], 71), 0),
        "prefix_len": draw_prefix_len(jax.random.fold_in(streams_of[18], 71), 0),
        "suffix_len": draw_suffix_len(jax.random.fold_in(streams_of[18], 71), 0),
        "request_group": draw_request_group(jax.random.fold_in(streams_of[18], 71), 0),
    }


EPSILON = 1e-06
THETA = 1000000.0
NEGATIVE = -1e+30

def rms_scale(values, gain):
    mean_square = lax.optimization_barrier(jnp.mean(values * values, axis=-1, keepdims=True))
    return values * lax.rsqrt(mean_square + EPSILON) * gain

def rotate(values, positions):
    half = values.shape[-1] // 2
    freqs = THETA ** (-jnp.arange(half).astype(jnp.float32) * 2.0 / values.shape[-1])
    angles = positions.astype(jnp.float32)[:, None] * freqs[None, :]
    angles = jnp.concatenate([angles, angles], axis=-1)
    cosine = jnp.cos(angles)[:, None, :]
    sine = jnp.sin(angles)[:, None, :]
    turned = jnp.concatenate([-values[..., half:], values[..., :half]], axis=-1)
    return values * cosine + turned * sine

def expert_apply(rows, gate_part, lift_part, down_part):
    gate_val = jnp.dot(rows, gate_part, preferred_element_type=jnp.float32)
    lift_val = jnp.dot(rows, lift_part, preferred_element_type=jnp.float32)
    hidden_units = (jax.nn.silu(gate_val) * lift_val).astype(jnp.bfloat16)
    return jnp.dot(hidden_units, down_part, preferred_element_type=jnp.float32)

def reference(residual_in, attn_gain, query_weight, kv_weight, query_gain, key_gain, out_weight, moe_gain, gate_weight, lift_weight, down_weight, routes, route_weights, prefix_cache, suffix_cache, prefix_len, suffix_len, request_group):
    normed = rms_scale(residual_in.astype(jnp.float32), attn_gain).astype(jnp.bfloat16)
    query_raw = jnp.dot(normed, query_weight, preferred_element_type=jnp.float32).reshape(TOKENS, HEADS, HD)
    kv_raw = jnp.dot(normed, kv_weight, preferred_element_type=jnp.float32).reshape(TOKENS, 2 * KVH, HD)
    positions = prefix_len[request_group] + suffix_len
    queries = rotate(rms_scale(query_raw, query_gain), positions).astype(jnp.bfloat16)
    new_keys = rotate(rms_scale(kv_raw[:, :KVH], key_gain), positions).astype(jnp.bfloat16)
    new_values = kv_raw[:, KVH:].astype(jnp.bfloat16)
    new_cache_rows = jnp.concatenate([new_keys, new_values], axis=1).reshape(TOKENS, 2 * KVH * HD)
    per_group = HEADS // KVH
    span = PRE + SUF + 1
    slot_index = jnp.arange(span)

    def attend(items):
        query, own_row, suffix_rows, group, suf_count = items
        pre_rows = lax.dynamic_index_in_dim(prefix_cache, group, 0, keepdims=False)
        pre_count = prefix_len[group]
        keys_all = jnp.concatenate([pre_rows, suffix_rows, own_row[None, :]], axis=0)
        key_part = keys_all[:, :KVH * HD].reshape(span, KVH, HD).astype(jnp.float32)
        value_part = keys_all[:, KVH * HD:].reshape(span, KVH, HD).astype(jnp.float32)
        query_f = query.reshape(KVH, per_group, HD).astype(jnp.float32)
        scores = jnp.einsum('gqd,sgd->gqs', query_f, key_part) / math.sqrt(HD)
        valid = jnp.where(slot_index < PRE, slot_index < pre_count, jnp.where(slot_index < PRE + SUF, slot_index - PRE < suf_count, True))
        highest = lax.optimization_barrier(jnp.max(jnp.where(valid, scores, NEGATIVE), axis=-1, keepdims=True))
        weights = jnp.where(valid, jnp.exp(scores - highest), 0.0)
        total = lax.optimization_barrier(jnp.sum(weights, axis=-1, keepdims=True))
        weights_low = lax.optimization_barrier(weights.astype(jnp.bfloat16)).astype(jnp.float32)
        mixed = jnp.einsum('gqs,sgd->gqd', weights_low, value_part, precision=lax.Precision.HIGHEST) / total
        return mixed.reshape(HEADS * HD).astype(jnp.bfloat16)
    attn_heads = lax.map(attend, (queries, new_cache_rows, suffix_cache, request_group, suffix_len))
    attn_out = jnp.dot(attn_heads, out_weight, preferred_element_type=jnp.float32)
    middle = (residual_in.astype(jnp.float32) + attn_out).astype(jnp.bfloat16)
    moe_in = rms_scale(middle.astype(jnp.float32), moe_gain).astype(jnp.bfloat16)
    share = route_weights / lax.optimization_barrier(jnp.sum(route_weights, axis=1, keepdims=True))
    limit = N_DP * CAP

    def add_expert(total_out, expert):
        hits = routes == expert
        chosen = jnp.any(hits, axis=1)
        picked = jnp.nonzero(chosen, size=limit, fill_value=0)[0].astype(jnp.int32)
        live = jnp.arange(limit) < jnp.sum(chosen.astype(jnp.int32))
        rows = moe_in[picked]
        outputs = expert_apply(rows, gate_weight[expert], lift_weight[expert], down_weight[expert])
        factor = lax.optimization_barrier(jnp.sum(jnp.where(hits, share, 0.0), axis=1))[picked]
        factor = jnp.where(live, factor, 0.0)
        return (total_out.at[picked].add(factor[:, None] * outputs), None)
    moe_out, unused = lax.scan(add_expert, jnp.zeros((TOKENS, D), jnp.float32), jnp.arange(EXPERTS).astype(jnp.int32))
    layer_out = (middle.astype(jnp.float32) + moe_out).astype(jnp.bfloat16)
    return (layer_out, new_cache_rows)
```

```python
import math

import jax
import jax.numpy as jnp
from jax import lax
from jax.sharding import PartitionSpec as P

EPSILON = 1e-06
THETA = 1000000.0
NEGATIVE = -1e30


def rms_scale(values, gain):
    mean_square = jnp.mean(values * values, axis=-1, keepdims=True)
    return values * lax.rsqrt(mean_square + EPSILON) * gain


def rotate(values, positions):
    half = values.shape[-1] // 2
    freqs = THETA ** (-jnp.arange(half).astype(jnp.float32) * 2.0 / values.shape[-1])
    angles = positions.astype(jnp.float32)[:, None] * freqs[None, :]
    angles = jnp.concatenate([angles, angles], axis=-1)
    cosine = jnp.cos(angles)[:, None, :]
    sine = jnp.sin(angles)[:, None, :]
    turned = jnp.concatenate([-values[..., half:], values[..., :half]], axis=-1)
    return values * cosine + turned * sine


def body(
    residual_in,
    attn_gain,
    query_weight,
    kv_weight,
    query_gain,
    key_gain,
    out_weight,
    moe_gain,
    gate_weight,
    lift_weight,
    down_weight,
    routes,
    route_weights,
    prefix_cache,
    suffix_cache,
    prefix_len,
    suffix_len,
    request_group,
):
    tensor_size = lax.axis_size("tensor")
    tensor_rank = lax.axis_index("tensor")
    dp_rank = lax.axis_index("dp")
    owners = lax.axis_size("dp")
    head_dim = query_gain.shape[0]
    requests = routes.shape[0]
    model_width = residual_in.shape[1]
    query_cols = query_weight.shape[1]
    kv_cols = kv_weight.shape[1]
    heads_here = query_cols // head_dim
    heads_all = heads_here * tensor_size
    kv_heads_all = kv_cols * tensor_size // (2 * head_dim)
    per_group = heads_all // kv_heads_all
    groups_dev = prefix_cache.shape[0]
    pre_local = prefix_cache.shape[1]
    suf_local = suffix_cache.shape[1]
    normed = rms_scale(residual_in.astype(jnp.float32), attn_gain).astype(jnp.bfloat16)
    piece = lax.all_gather(normed, "tensor", axis=0, tiled=True)
    projected = jnp.concatenate(
        [
            jnp.dot(piece, query_weight, preferred_element_type=jnp.float32),
            jnp.dot(piece, kv_weight, preferred_element_type=jnp.float32),
        ],
        axis=1,
    )
    query_raw = projected[:, :query_cols].reshape(requests, heads_here, head_dim)
    kv_raw = projected[:, query_cols:].reshape(requests, kv_cols // head_dim, head_dim)
    group_ids = dp_rank * groups_dev + jnp.arange(groups_dev)
    member = request_group[:, None] == group_ids[None, :]
    prefix_of = jnp.sum(jnp.where(member, prefix_len[None, :], 0), axis=1)
    positions = prefix_of + suffix_len
    queries = rotate(rms_scale(query_raw, query_gain), positions).astype(jnp.bfloat16)
    head_number = tensor_rank * (kv_cols // head_dim) + jnp.arange(kv_cols // head_dim)
    is_key = (head_number < kv_heads_all)[None, :, None]
    keyed = rotate(rms_scale(kv_raw, key_gain), positions)
    new_rows = jnp.where(is_key, keyed, kv_raw).astype(jnp.bfloat16).reshape(requests, kv_cols)
    joined = jnp.concatenate([queries.reshape(requests, query_cols), new_rows], axis=1)
    every_head = lax.all_gather(joined, "tensor", axis=1, tiled=True).reshape(
        requests, tensor_size, query_cols + kv_cols
    )
    all_queries = every_head[:, :, :query_cols].reshape(requests, kv_heads_all, per_group, head_dim)
    all_kv = every_head[:, :, query_cols:]
    own_keys = all_kv[:, :kv_heads_all]
    own_values = all_kv[:, kv_heads_all:].astype(jnp.float32)
    scale = 1.0 / math.sqrt(head_dim)
    split_at = kv_heads_all * head_dim
    pre_keys = prefix_cache[:, :, :split_at].reshape(groups_dev, pre_local, kv_heads_all, head_dim)
    pre_values = prefix_cache[:, :, split_at:].reshape(
        groups_dev, pre_local, kv_heads_all, head_dim
    )
    suf_keys = suffix_cache[:, :, :split_at].reshape(requests, suf_local, kv_heads_all, head_dim)
    suf_values = suffix_cache[:, :, split_at:].reshape(requests, suf_local, kv_heads_all, head_dim)
    pre_scores = (
        jnp.einsum("rgqd,npgd->rgqnp", all_queries, pre_keys, preferred_element_type=jnp.float32)
        * scale
    )
    suf_scores = (
        jnp.einsum("rgqd,rsgd->rgqs", all_queries, suf_keys, preferred_element_type=jnp.float32)
        * scale
    )
    own_scores = (
        jnp.einsum("rgqd,rgd->rgq", all_queries, own_keys, preferred_element_type=jnp.float32)
        * scale
    )
    pre_slots = tensor_rank * pre_local + jnp.arange(pre_local)
    pre_valid = (member[:, :, None] & (pre_slots[None, None, :] < prefix_len[None, :, None]))[
        :, None, None, :, :
    ]
    suf_slots = tensor_rank * suf_local + jnp.arange(suf_local)
    suf_valid = (suf_slots[None, :] < suffix_len[:, None])[:, None, None, :]
    own_valid = tensor_rank == 0
    top_pre = jnp.max(jnp.where(pre_valid, pre_scores, NEGATIVE), axis=(3, 4))
    top_suf = jnp.max(jnp.where(suf_valid, suf_scores, NEGATIVE), axis=3)
    top_own = jnp.where(own_valid, own_scores, NEGATIVE)
    top_local = jnp.maximum(jnp.maximum(top_pre, top_suf), top_own)
    pre_weights = jnp.where(pre_valid, jnp.exp(pre_scores - top_local[..., None, None]), 0.0)
    suf_weights = jnp.where(suf_valid, jnp.exp(suf_scores - top_local[..., None]), 0.0)
    own_weights = jnp.where(own_valid, jnp.exp(own_scores - top_local), 0.0)
    total_local = jnp.sum(pre_weights, axis=(3, 4)) + jnp.sum(suf_weights, axis=3) + own_weights
    sums_local = jnp.einsum(
        "rgqnp,npgd->rgqd",
        pre_weights.astype(jnp.bfloat16),
        pre_values,
        preferred_element_type=jnp.float32,
    )
    sums_local = sums_local + jnp.einsum(
        "rgqs,rsgd->rgqd",
        suf_weights.astype(jnp.bfloat16),
        suf_values,
        preferred_element_type=jnp.float32,
    )
    own_low = own_weights.astype(jnp.bfloat16).astype(jnp.float32)
    sums_local = sums_local + own_low[..., None] * own_values[:, :, None, :]
    packed = jnp.concatenate(
        [
            sums_local.reshape(requests, heads_all, head_dim),
            top_local.reshape(requests, heads_all, 1),
            total_local.reshape(requests, heads_all, 1),
        ],
        axis=2,
    )
    packed = packed.reshape(requests, tensor_size, heads_here, head_dim + 2).transpose(1, 0, 2, 3)
    parts = lax.all_to_all(packed, "tensor", 0, 0, tiled=True)
    part_sums = parts[..., :head_dim]
    part_top = parts[..., head_dim]
    part_total = parts[..., head_dim + 1]
    top_all = jnp.max(part_top, axis=0)
    factor = jnp.exp(part_top - top_all[None])
    total_mine = jnp.sum(part_total * factor, axis=0)
    sums_mine = jnp.sum(part_sums * factor[..., None], axis=0)
    mixed = sums_mine / total_mine[..., None]
    attn_heads = mixed.reshape(requests, query_cols).astype(jnp.bfloat16)
    attn_out = lax.psum_scatter(
        jnp.dot(attn_heads, out_weight, preferred_element_type=jnp.float32).astype(jnp.bfloat16),
        "tensor",
        scatter_dimension=0,
        tiled=True,
    ).astype(jnp.float32)
    middle = (residual_in.astype(jnp.float32) + attn_out).astype(jnp.bfloat16)
    moe_in = rms_scale(middle.astype(jnp.float32), moe_gain).astype(jnp.bfloat16)
    local_experts = gate_weight.shape[0]
    experts_all = local_experts * owners
    topk = routes.shape[1]
    capacity = 2 * requests * topk // experts_all
    flat_routes = routes.reshape(-1)
    onehot = (flat_routes[:, None] == jnp.arange(experts_all)[None, :]).astype(jnp.int32)
    running = jnp.cumsum(onehot, axis=0)
    slot_of = jnp.sum(onehot * running, axis=1) - 1
    code_of = (flat_routes * capacity + slot_of).reshape(requests, topk)
    code_span = jnp.arange(experts_all * capacity)
    placing = jnp.any(code_of[None, :, :] == code_span[:, None, None], axis=2).astype(jnp.bfloat16)
    share = route_weights / jnp.sum(route_weights, axis=1, keepdims=True)
    width_here = model_width // tensor_size
    gathered_in = lax.all_gather(moe_in, "tensor", axis=0, tiled=True)
    cols_in = lax.dynamic_slice_in_dim(gathered_in, tensor_rank * width_here, width_here, 1)
    placed = jnp.dot(placing, cols_in, preferred_element_type=jnp.float32)
    outgoing = placed.astype(jnp.bfloat16).reshape(owners, local_experts * capacity, width_here)
    arrived = lax.all_to_all(outgoing, "dp", split_axis=0, concat_axis=0, tiled=True)
    rows = lax.all_gather(arrived, "tensor", axis=2, tiled=True).reshape(
        owners, local_experts, capacity, model_width
    )
    gate_val = jnp.einsum("necd,edf->necf", rows, gate_weight, preferred_element_type=jnp.float32)
    lift_val = jnp.einsum("necd,edf->necf", rows, lift_weight, preferred_element_type=jnp.float32)
    hidden_units = (jax.nn.silu(gate_val) * lift_val).astype(jnp.bfloat16)
    partial_out = jnp.einsum(
        "necf,efd->necd", hidden_units, down_weight, preferred_element_type=jnp.float32
    ).astype(jnp.bfloat16)
    summed_out = lax.psum_scatter(partial_out, "tensor", scatter_dimension=3, tiled=True)
    returned = lax.all_to_all(
        summed_out.reshape(owners, local_experts * capacity, width_here),
        "dp",
        split_axis=0,
        concat_axis=0,
        tiled=True,
    ).astype(jnp.float32)
    returned = returned.reshape(experts_all * capacity, width_here)
    picked_rows = returned[code_of]
    moe_cols = jnp.sum(share[:, :, None] * picked_rows, axis=1).astype(jnp.bfloat16)
    moe_out = lax.all_to_all(moe_cols, "tensor", split_axis=0, concat_axis=1, tiled=True).astype(
        jnp.float32
    )
    layer_out = (middle.astype(jnp.float32) + moe_out).astype(jnp.bfloat16)
    return (layer_out, new_rows)


def solution(mesh):
    in_specs = (
        P(("dp", "tensor"), None),
        P(),
        P(None, "tensor"),
        P(None, "tensor"),
        P(),
        P(),
        P("tensor", None),
        P(),
        P("dp", None, "tensor"),
        P("dp", None, "tensor"),
        P("dp", "tensor", None),
        P("dp", None),
        P("dp", None),
        P("dp", "tensor", None),
        P("dp", "tensor", None),
        P("dp"),
        P("dp"),
        P("dp"),
    )
    out_specs = (P(("dp", "tensor"), None), P("dp", "tensor"))
    return jax.shard_map(body, mesh=mesh, in_specs=in_specs, out_specs=out_specs, check_vma=False)
```

```python
import math

import jax
import jax.numpy as jnp
from jax import lax
from jax.sharding import Mesh, PartitionSpec as P

EPSILON = 1e-06
THETA = 1000000.0
NEGATIVE = -1e30
TENSOR = ("tx", "tc")


def rms_scale(values, gain):
    mean_square = jnp.mean(values * values, axis=-1, keepdims=True)
    return values * lax.rsqrt(mean_square + EPSILON) * gain


def rotate(values, positions):
    half = values.shape[-1] // 2
    freqs = THETA ** (-jnp.arange(half).astype(jnp.float32) * 2.0 / values.shape[-1])
    angles = positions.astype(jnp.float32)[:, None] * freqs[None, :]
    angles = jnp.concatenate([angles, angles], axis=-1)
    cosine = jnp.cos(angles)[:, None, :]
    sine = jnp.sin(angles)[:, None, :]
    turned = jnp.concatenate([-values[..., half:], values[..., :half]], axis=-1)
    return values * cosine + turned * sine


def body(
    residual_in,
    attn_gain,
    query_weight,
    kv_weight,
    query_gain,
    key_gain,
    out_weight,
    moe_gain,
    gate_weight,
    lift_weight,
    down_weight,
    routes,
    route_weights,
    prefix_cache,
    suffix_cache,
    prefix_len,
    suffix_len,
    request_group,
):
    tensor_size = lax.axis_size(TENSOR)
    chip_rank = lax.axis_index("tx")
    core_rank = lax.axis_index("tc")
    chips = lax.axis_size("tx")
    tensor_rank = chip_rank * lax.axis_size("tc") + core_rank
    chunk_rank = core_rank * chips + chip_rank
    dp_rank = lax.axis_index("dp")
    owners = lax.axis_size("dp")
    head_dim = query_gain.shape[0]
    requests = routes.shape[0]
    model_width = residual_in.shape[1]
    query_cols = query_weight.shape[1]
    kv_cols = kv_weight.shape[1]
    heads_here = query_cols // head_dim
    heads_all = heads_here * tensor_size
    kv_heads_all = kv_cols * tensor_size // (2 * head_dim)
    per_group = heads_all // kv_heads_all
    groups_dev = prefix_cache.shape[0]
    pre_local = prefix_cache.shape[1]
    suf_local = suffix_cache.shape[1]
    residual_all = lax.all_gather(residual_in, TENSOR, axis=0, tiled=True)
    piece = rms_scale(residual_all.astype(jnp.float32), attn_gain).astype(jnp.bfloat16)
    projected = jnp.concatenate(
        [
            jnp.dot(piece, query_weight, preferred_element_type=jnp.float32),
            jnp.dot(piece, kv_weight, preferred_element_type=jnp.float32),
        ],
        axis=1,
    )
    query_raw = projected[:, :query_cols].reshape(requests, heads_here, head_dim)
    kv_raw = projected[:, query_cols:].reshape(requests, kv_cols // head_dim, head_dim)
    group_ids = dp_rank * groups_dev + jnp.arange(groups_dev)
    member = request_group[:, None] == group_ids[None, :]
    prefix_of = jnp.sum(jnp.where(member, prefix_len[None, :], 0), axis=1)
    positions = prefix_of + suffix_len
    queries = rotate(rms_scale(query_raw, query_gain), positions).astype(jnp.bfloat16)
    head_number = tensor_rank * (kv_cols // head_dim) + jnp.arange(kv_cols // head_dim)
    is_key = (head_number < kv_heads_all)[None, :, None]
    keyed = rotate(rms_scale(kv_raw, key_gain), positions)
    new_rows = jnp.where(is_key, keyed, kv_raw).astype(jnp.bfloat16).reshape(requests, kv_cols)
    joined = jnp.concatenate([queries.reshape(requests, query_cols), new_rows], axis=1)
    every_head = lax.all_gather(joined, TENSOR, axis=1, tiled=True).reshape(
        requests, tensor_size, query_cols + kv_cols
    )
    all_queries = every_head[:, :, :query_cols].reshape(requests, kv_heads_all, per_group, head_dim)
    all_kv = every_head[:, :, query_cols:]
    own_keys = all_kv[:, :kv_heads_all]
    own_values = all_kv[:, kv_heads_all:].astype(jnp.float32)
    scale = 1.0 / math.sqrt(head_dim)
    split_at = kv_heads_all * head_dim
    pre_keys = prefix_cache[:, :, :split_at].reshape(groups_dev, pre_local, kv_heads_all, head_dim)
    pre_values = prefix_cache[:, :, split_at:].reshape(
        groups_dev, pre_local, kv_heads_all, head_dim
    )
    suf_keys = suffix_cache[:, :, :split_at].reshape(requests, suf_local, kv_heads_all, head_dim)
    suf_values = suffix_cache[:, :, split_at:].reshape(requests, suf_local, kv_heads_all, head_dim)
    pre_scores = (
        jnp.einsum("rgqd,npgd->rgqnp", all_queries, pre_keys, preferred_element_type=jnp.float32)
        * scale
    )
    suf_scores = (
        jnp.einsum("rgqd,rsgd->rgqs", all_queries, suf_keys, preferred_element_type=jnp.float32)
        * scale
    )
    own_scores = (
        jnp.einsum("rgqd,rgd->rgq", all_queries, own_keys, preferred_element_type=jnp.float32)
        * scale
    )
    pre_slots = tensor_rank * pre_local + jnp.arange(pre_local)
    pre_valid = (member[:, :, None] & (pre_slots[None, None, :] < prefix_len[None, :, None]))[
        :, None, None, :, :
    ]
    suf_slots = tensor_rank * suf_local + jnp.arange(suf_local)
    suf_valid = (suf_slots[None, :] < suffix_len[:, None])[:, None, None, :]
    own_valid = tensor_rank == 0
    top_pre = jnp.max(jnp.where(pre_valid, pre_scores, NEGATIVE), axis=(3, 4))
    top_suf = jnp.max(jnp.where(suf_valid, suf_scores, NEGATIVE), axis=3)
    top_own = jnp.where(own_valid, own_scores, NEGATIVE)
    top_local = jnp.maximum(jnp.maximum(top_pre, top_suf), top_own)
    pre_weights = jnp.where(pre_valid, jnp.exp(pre_scores - top_local[..., None, None]), 0.0)
    suf_weights = jnp.where(suf_valid, jnp.exp(suf_scores - top_local[..., None]), 0.0)
    own_weights = jnp.where(own_valid, jnp.exp(own_scores - top_local), 0.0)
    total_local = jnp.sum(pre_weights, axis=(3, 4)) + jnp.sum(suf_weights, axis=3) + own_weights
    sums_local = jnp.einsum(
        "rgqnp,npgd->rgqd",
        pre_weights.astype(jnp.bfloat16),
        pre_values,
        preferred_element_type=jnp.float32,
    )
    sums_local = sums_local + jnp.einsum(
        "rgqs,rsgd->rgqd",
        suf_weights.astype(jnp.bfloat16),
        suf_values,
        preferred_element_type=jnp.float32,
    )
    own_low = own_weights.astype(jnp.bfloat16).astype(jnp.float32)
    sums_local = sums_local + own_low[..., None] * own_values[:, :, None, :]
    packed = jnp.concatenate(
        [
            sums_local.reshape(requests, heads_all, head_dim),
            top_local.reshape(requests, heads_all, 1),
            total_local.reshape(requests, heads_all, 1),
        ],
        axis=2,
    )
    packed = packed.reshape(requests, tensor_size, heads_here, head_dim + 2).transpose(1, 0, 2, 3)
    parts = lax.all_to_all(packed, TENSOR, 0, 0, tiled=True)
    part_sums = parts[..., :head_dim]
    part_top = parts[..., head_dim]
    part_total = parts[..., head_dim + 1]
    top_all = jnp.max(part_top, axis=0)
    factor = jnp.exp(part_top - top_all[None])
    total_mine = jnp.sum(part_total * factor, axis=0)
    sums_mine = jnp.sum(part_sums * factor[..., None], axis=0)
    mixed = sums_mine / total_mine[..., None]
    attn_heads = mixed.reshape(requests, query_cols).astype(jnp.bfloat16)
    attn_all = lax.psum(
        jnp.dot(attn_heads, out_weight, preferred_element_type=jnp.float32), TENSOR
    )
    middle_all = (residual_all.astype(jnp.float32) + attn_all).astype(jnp.bfloat16)
    tokens_here = residual_in.shape[0]
    middle = lax.dynamic_slice_in_dim(middle_all, tensor_rank * tokens_here, tokens_here, 0)
    moe_all = rms_scale(middle_all.astype(jnp.float32), moe_gain).astype(jnp.bfloat16)
    local_experts = gate_weight.shape[0]
    experts_all = local_experts * owners
    topk = routes.shape[1]
    capacity = 2 * requests * topk // experts_all
    flat_routes = routes.reshape(-1)
    onehot = (flat_routes[:, None] == jnp.arange(experts_all)[None, :]).astype(jnp.int32)
    running = jnp.cumsum(onehot, axis=0)
    slot_of = jnp.sum(onehot * running, axis=1) - 1
    code_of = (flat_routes * capacity + slot_of).reshape(requests, topk)
    code_span = jnp.arange(experts_all * capacity)
    placing = jnp.any(code_of[None, :, :] == code_span[:, None, None], axis=2).astype(jnp.bfloat16)
    share = route_weights / jnp.sum(route_weights, axis=1, keepdims=True)
    width_here = model_width // tensor_size
    cols_in = lax.dynamic_slice_in_dim(moe_all, chunk_rank * width_here, width_here, 1)
    placed = jnp.dot(placing, cols_in, preferred_element_type=jnp.float32)
    outgoing = placed.astype(jnp.bfloat16).reshape(owners, local_experts * capacity, width_here)
    arrived = lax.all_to_all(outgoing, "dp", split_axis=0, concat_axis=0, tiled=True)
    half_rows = lax.all_gather(arrived, "tx", axis=2, tiled=True)
    rows = lax.all_gather(half_rows, "tc", axis=2, tiled=True).reshape(
        owners, local_experts, capacity, model_width
    )
    gate_val = jnp.einsum("necd,edf->necf", rows, gate_weight, preferred_element_type=jnp.float32)
    lift_val = jnp.einsum("necd,edf->necf", rows, lift_weight, preferred_element_type=jnp.float32)
    hidden_units = (jax.nn.silu(gate_val) * lift_val).astype(jnp.bfloat16)
    partial_out = jnp.einsum(
        "necf,efd->necd", hidden_units, down_weight, preferred_element_type=jnp.float32
    ).astype(jnp.bfloat16)
    core_out = lax.psum_scatter(partial_out, "tc", scatter_dimension=3, tiled=True)
    summed_out = lax.psum_scatter(core_out, "tx", scatter_dimension=3, tiled=True)
    returned = lax.all_to_all(
        summed_out.reshape(owners, local_experts * capacity, width_here),
        "dp",
        split_axis=0,
        concat_axis=0,
        tiled=True,
    ).astype(jnp.float32)
    returned = returned.reshape(experts_all * capacity, width_here)
    picked_rows = returned[code_of]
    moe_cols = jnp.sum(share[:, :, None] * picked_rows, axis=1).astype(jnp.bfloat16)
    moe_chunks = lax.all_to_all(moe_cols, TENSOR, split_axis=0, concat_axis=1, tiled=True)
    moe_out = (
        moe_chunks.reshape(tokens_here, chips, tensor_size // chips, width_here)
        .transpose(0, 2, 1, 3)
        .reshape(tokens_here, model_width)
        .astype(jnp.float32)
    )
    layer_out = (middle.astype(jnp.float32) + moe_out).astype(jnp.bfloat16)
    return (layer_out, new_rows)


def solution(mesh):
    cores = mesh.devices.shape[1] // 2
    split_mesh = Mesh(mesh.devices.reshape(mesh.devices.shape[0], cores, 2), ("dp", "tx", "tc"))
    in_specs = (
        P(("dp", "tx", "tc"), None),
        P(),
        P(None, TENSOR),
        P(None, TENSOR),
        P(),
        P(),
        P(TENSOR, None),
        P(),
        P("dp", None, TENSOR),
        P("dp", None, TENSOR),
        P("dp", TENSOR, None),
        P("dp", None),
        P("dp", None),
        P("dp", TENSOR, None),
        P("dp", TENSOR, None),
        P("dp"),
        P("dp"),
        P("dp"),
    )
    out_specs = (P(("dp", "tx", "tc"), None), P("dp", TENSOR))
    return jax.shard_map(body, mesh=split_mesh, in_specs=in_specs, out_specs=out_specs, check_vma=False)
```

```python
import math

import jax
import jax.numpy as jnp
from jax import lax
from jax.sharding import PartitionSpec as P

EPSILON = 1e-06
THETA = 1000000.0
NEGATIVE = -1e30


def rms_scale(values, gain):
    mean_square = jnp.mean(values * values, axis=-1, keepdims=True)
    return values * lax.rsqrt(mean_square + EPSILON) * gain


def rotate(values, positions):
    half = values.shape[-1] // 2
    freqs = THETA ** (-jnp.arange(half).astype(jnp.float32) * 2.0 / values.shape[-1])
    angles = positions.astype(jnp.float32)[:, None] * freqs[None, :]
    angles = jnp.concatenate([angles, angles], axis=-1)
    cosine = jnp.cos(angles)[:, None, :]
    sine = jnp.sin(angles)[:, None, :]
    turned = jnp.concatenate([-values[..., half:], values[..., :half]], axis=-1)
    return values * cosine + turned * sine


def body(
    residual_in,
    attn_gain,
    query_weight,
    kv_weight,
    query_gain,
    key_gain,
    out_weight,
    moe_gain,
    gate_weight,
    lift_weight,
    down_weight,
    routes,
    route_weights,
    prefix_cache,
    suffix_cache,
    prefix_len,
    suffix_len,
    request_group,
):
    tensor_size = lax.axis_size("tensor")
    tensor_rank = lax.axis_index("tensor")
    dp_rank = lax.axis_index("dp")
    owners = lax.axis_size("dp")
    head_dim = query_gain.shape[0]
    requests = routes.shape[0]
    model_width = residual_in.shape[1]
    query_cols = query_weight.shape[1]
    kv_cols = kv_weight.shape[1]
    heads_here = query_cols // head_dim
    heads_all = heads_here * tensor_size
    kv_heads_all = kv_cols * tensor_size // (2 * head_dim)
    per_group = heads_all // kv_heads_all
    groups_dev = prefix_cache.shape[0]
    pre_local = prefix_cache.shape[1]
    suf_local = suffix_cache.shape[1]
    residual_all = lax.all_gather(residual_in, "tensor", axis=0, tiled=True)
    piece = rms_scale(residual_all.astype(jnp.float32), attn_gain).astype(jnp.bfloat16)
    projected = jnp.concatenate(
        [
            jnp.dot(piece, query_weight, preferred_element_type=jnp.float32),
            jnp.dot(piece, kv_weight, preferred_element_type=jnp.float32),
        ],
        axis=1,
    )
    query_raw = projected[:, :query_cols].reshape(requests, heads_here, head_dim)
    kv_raw = projected[:, query_cols:].reshape(requests, kv_cols // head_dim, head_dim)
    group_ids = dp_rank * groups_dev + jnp.arange(groups_dev)
    member = request_group[:, None] == group_ids[None, :]
    prefix_of = jnp.sum(jnp.where(member, prefix_len[None, :], 0), axis=1)
    positions = prefix_of + suffix_len
    queries = rotate(rms_scale(query_raw, query_gain), positions).astype(jnp.bfloat16)
    head_number = tensor_rank * (kv_cols // head_dim) + jnp.arange(kv_cols // head_dim)
    is_key = (head_number < kv_heads_all)[None, :, None]
    keyed = rotate(rms_scale(kv_raw, key_gain), positions)
    new_rows = jnp.where(is_key, keyed, kv_raw).astype(jnp.bfloat16).reshape(requests, kv_cols)
    joined = jnp.concatenate([queries.reshape(requests, query_cols), new_rows], axis=1)
    every_head = lax.all_gather(joined, "tensor", axis=1, tiled=True).reshape(
        requests, tensor_size, query_cols + kv_cols
    )
    all_queries = every_head[:, :, :query_cols].reshape(requests, kv_heads_all, per_group, head_dim)
    all_kv = every_head[:, :, query_cols:]
    own_keys = all_kv[:, :kv_heads_all]
    own_values = all_kv[:, kv_heads_all:].astype(jnp.float32)
    scale = 1.0 / math.sqrt(head_dim)
    split_at = kv_heads_all * head_dim
    pre_keys = prefix_cache[:, :, :split_at].reshape(groups_dev, pre_local, kv_heads_all, head_dim)
    pre_values = prefix_cache[:, :, split_at:].reshape(
        groups_dev, pre_local, kv_heads_all, head_dim
    )
    suf_keys = suffix_cache[:, :, :split_at].reshape(requests, suf_local, kv_heads_all, head_dim)
    suf_values = suffix_cache[:, :, split_at:].reshape(requests, suf_local, kv_heads_all, head_dim)
    pre_scores = (
        jnp.einsum("rgqd,npgd->rgqnp", all_queries, pre_keys, preferred_element_type=jnp.float32)
        * scale
    )
    suf_scores = (
        jnp.einsum("rgqd,rsgd->rgqs", all_queries, suf_keys, preferred_element_type=jnp.float32)
        * scale
    )
    own_scores = (
        jnp.einsum("rgqd,rgd->rgq", all_queries, own_keys, preferred_element_type=jnp.float32)
        * scale
    )
    pre_slots = tensor_rank * pre_local + jnp.arange(pre_local)
    pre_valid = (member[:, :, None] & (pre_slots[None, None, :] < prefix_len[None, :, None]))[
        :, None, None, :, :
    ]
    suf_slots = tensor_rank * suf_local + jnp.arange(suf_local)
    suf_valid = (suf_slots[None, :] < suffix_len[:, None])[:, None, None, :]
    own_valid = tensor_rank == 0
    top_pre = jnp.max(jnp.where(pre_valid, pre_scores, NEGATIVE), axis=(3, 4))
    top_suf = jnp.max(jnp.where(suf_valid, suf_scores, NEGATIVE), axis=3)
    top_own = jnp.where(own_valid, own_scores, NEGATIVE)
    top_local = jnp.maximum(jnp.maximum(top_pre, top_suf), top_own)
    pre_weights = jnp.where(pre_valid, jnp.exp(pre_scores - top_local[..., None, None]), 0.0)
    suf_weights = jnp.where(suf_valid, jnp.exp(suf_scores - top_local[..., None]), 0.0)
    own_weights = jnp.where(own_valid, jnp.exp(own_scores - top_local), 0.0)
    total_local = jnp.sum(pre_weights, axis=(3, 4)) + jnp.sum(suf_weights, axis=3) + own_weights
    sums_local = jnp.einsum(
        "rgqnp,npgd->rgqd",
        pre_weights.astype(jnp.bfloat16),
        pre_values,
        preferred_element_type=jnp.float32,
    )
    sums_local = sums_local + jnp.einsum(
        "rgqs,rsgd->rgqd",
        suf_weights.astype(jnp.bfloat16),
        suf_values,
        preferred_element_type=jnp.float32,
    )
    own_low = own_weights.astype(jnp.bfloat16).astype(jnp.float32)
    sums_local = sums_local + own_low[..., None] * own_values[:, :, None, :]
    packed = jnp.concatenate(
        [
            sums_local.reshape(requests, heads_all, head_dim),
            top_local.reshape(requests, heads_all, 1),
            total_local.reshape(requests, heads_all, 1),
        ],
        axis=2,
    )
    packed = packed.reshape(requests, tensor_size, heads_here, head_dim + 2).transpose(1, 0, 2, 3)
    parts = lax.all_to_all(packed, "tensor", 0, 0, tiled=True)
    part_sums = parts[..., :head_dim]
    part_top = parts[..., head_dim]
    part_total = parts[..., head_dim + 1]
    top_all = jnp.max(part_top, axis=0)
    factor = jnp.exp(part_top - top_all[None])
    total_mine = jnp.sum(part_total * factor, axis=0)
    sums_mine = jnp.sum(part_sums * factor[..., None], axis=0)
    mixed = sums_mine / total_mine[..., None]
    attn_heads = mixed.reshape(requests, query_cols).astype(jnp.bfloat16)
    width_here = model_width // tensor_size
    tokens_here = residual_in.shape[0]
    attn_parts = lax.all_to_all(
        jnp.dot(attn_heads, out_weight, preferred_element_type=jnp.float32).astype(jnp.bfloat16),
        "tensor",
        split_axis=1,
        concat_axis=0,
        tiled=True,
    ).reshape(tensor_size, requests, width_here)
    attn_cols = jnp.sum(attn_parts.astype(jnp.float32), axis=0)
    residual_cols = lax.dynamic_slice_in_dim(residual_all, tensor_rank * width_here, width_here, 1)
    middle_cols = (residual_cols.astype(jnp.float32) + attn_cols).astype(jnp.bfloat16)
    middle_wide = middle_cols.astype(jnp.float32)
    square_sum = lax.psum(jnp.sum(middle_wide * middle_wide, axis=1, keepdims=True), "tensor")
    gain_cols = lax.dynamic_slice_in_dim(moe_gain, tensor_rank * width_here, width_here, 0)
    cols_in = (
        middle_wide * lax.rsqrt(square_sum / model_width + EPSILON) * gain_cols
    ).astype(jnp.bfloat16)
    local_experts = gate_weight.shape[0]
    experts_all = local_experts * owners
    topk = routes.shape[1]
    capacity = 2 * requests * topk // experts_all
    flat_routes = routes.reshape(-1)
    onehot = (flat_routes[:, None] == jnp.arange(experts_all)[None, :]).astype(jnp.int32)
    running = jnp.cumsum(onehot, axis=0)
    slot_of = jnp.sum(onehot * running, axis=1) - 1
    code_of = (flat_routes * capacity + slot_of).reshape(requests, topk)
    code_span = jnp.arange(experts_all * capacity)
    placing = jnp.any(code_of[None, :, :] == code_span[:, None, None], axis=2).astype(jnp.bfloat16)
    share = route_weights / jnp.sum(route_weights, axis=1, keepdims=True)
    placed = jnp.dot(placing, cols_in, preferred_element_type=jnp.float32)
    outgoing = placed.astype(jnp.bfloat16).reshape(owners, local_experts * capacity, width_here)
    arrived = lax.all_to_all(outgoing, "dp", split_axis=0, concat_axis=0, tiled=True)
    rows = lax.all_gather(arrived, "tensor", axis=2, tiled=True).reshape(
        owners, local_experts, capacity, model_width
    )
    gate_val = jnp.einsum("necd,edf->necf", rows, gate_weight, preferred_element_type=jnp.float32)
    lift_val = jnp.einsum("necd,edf->necf", rows, lift_weight, preferred_element_type=jnp.float32)
    hidden_units = (jax.nn.silu(gate_val) * lift_val).astype(jnp.bfloat16)
    partial_out = jnp.einsum(
        "necf,efd->necd", hidden_units, down_weight, preferred_element_type=jnp.float32
    ).astype(jnp.bfloat16)
    summed_out = lax.psum_scatter(partial_out, "tensor", scatter_dimension=3, tiled=True)
    returned = lax.all_to_all(
        summed_out.reshape(owners, local_experts * capacity, width_here),
        "dp",
        split_axis=0,
        concat_axis=0,
        tiled=True,
    ).astype(jnp.float32)
    returned = returned.reshape(experts_all * capacity, width_here)
    picked_rows = returned[code_of]
    moe_cols = jnp.sum(share[:, :, None] * picked_rows, axis=1)
    layer_cols = (middle_wide + moe_cols).astype(jnp.bfloat16)
    layer_out = lax.all_to_all(layer_cols, "tensor", split_axis=0, concat_axis=1, tiled=True)
    return (layer_out, new_rows)


def solution(mesh):
    in_specs = (
        P(("dp", "tensor"), None),
        P(),
        P(None, "tensor"),
        P(None, "tensor"),
        P(),
        P(),
        P("tensor", None),
        P(),
        P("dp", None, "tensor"),
        P("dp", None, "tensor"),
        P("dp", "tensor", None),
        P("dp", None),
        P("dp", None),
        P("dp", "tensor", None),
        P("dp", "tensor", None),
        P("dp"),
        P("dp"),
        P("dp"),
    )
    out_specs = (P(("dp", "tensor"), None), P("dp", "tensor"))
    return jax.shard_map(body, mesh=mesh, in_specs=in_specs, out_specs=out_specs, check_vma=False)
```

```python
import math

import jax
import jax.numpy as jnp
from jax import lax
from jax.sharding import PartitionSpec as P

EPSILON = 1e-06
THETA = 1000000.0
NEGATIVE = -1e30


def rms_scale(values, gain):
    mean_square = jnp.mean(values * values, axis=-1, keepdims=True)
    return values * lax.rsqrt(mean_square + EPSILON) * gain


def rotate(values, positions):
    half = values.shape[-1] // 2
    freqs = THETA ** (-jnp.arange(half).astype(jnp.float32) * 2.0 / values.shape[-1])
    angles = positions.astype(jnp.float32)[:, None] * freqs[None, :]
    angles = jnp.concatenate([angles, angles], axis=-1)
    cosine = jnp.cos(angles)[:, None, :]
    sine = jnp.sin(angles)[:, None, :]
    turned = jnp.concatenate([-values[..., half:], values[..., :half]], axis=-1)
    return values * cosine + turned * sine


def body(
    residual_in,
    attn_gain,
    query_weight,
    kv_weight,
    query_gain,
    key_gain,
    out_weight,
    moe_gain,
    gate_weight,
    lift_weight,
    down_weight,
    routes,
    route_weights,
    prefix_cache,
    suffix_cache,
    prefix_len,
    suffix_len,
    request_group,
):
    tensor_size = lax.axis_size("tensor")
    tensor_rank = lax.axis_index("tensor")
    dp_rank = lax.axis_index("dp")
    owners = lax.axis_size("dp")
    head_dim = query_gain.shape[0]
    requests = routes.shape[0]
    model_width = residual_in.shape[1]
    query_cols = query_weight.shape[1]
    kv_cols = kv_weight.shape[1]
    heads_here = query_cols // head_dim
    heads_all = heads_here * tensor_size
    kv_heads_all = kv_cols * tensor_size // (2 * head_dim)
    per_group = heads_all // kv_heads_all
    groups_dev = prefix_cache.shape[0]
    pre_local = prefix_cache.shape[1]
    suf_local = suffix_cache.shape[1]
    residual_all = lax.all_gather(residual_in, "tensor", axis=0, tiled=True)
    piece = rms_scale(residual_all.astype(jnp.float32), attn_gain).astype(jnp.bfloat16)
    projected = jnp.concatenate(
        [
            jnp.dot(piece, query_weight, preferred_element_type=jnp.float32),
            jnp.dot(piece, kv_weight, preferred_element_type=jnp.float32),
        ],
        axis=1,
    )
    query_raw = projected[:, :query_cols].reshape(requests, heads_here, head_dim)
    kv_raw = projected[:, query_cols:].reshape(requests, kv_cols // head_dim, head_dim)
    group_ids = dp_rank * groups_dev + jnp.arange(groups_dev)
    member = request_group[:, None] == group_ids[None, :]
    prefix_of = jnp.sum(jnp.where(member, prefix_len[None, :], 0), axis=1)
    positions = prefix_of + suffix_len
    queries = rotate(rms_scale(query_raw, query_gain), positions).astype(jnp.bfloat16)
    head_number = tensor_rank * (kv_cols // head_dim) + jnp.arange(kv_cols // head_dim)
    is_key = (head_number < kv_heads_all)[None, :, None]
    keyed = rotate(rms_scale(kv_raw, key_gain), positions)
    new_rows = jnp.where(is_key, keyed, kv_raw).astype(jnp.bfloat16).reshape(requests, kv_cols)
    joined = jnp.concatenate([queries.reshape(requests, query_cols), new_rows], axis=1)
    every_head = lax.all_gather(joined, "tensor", axis=1, tiled=True).reshape(
        requests, tensor_size, query_cols + kv_cols
    )
    all_queries = every_head[:, :, :query_cols].reshape(requests, kv_heads_all, per_group, head_dim)
    all_kv = every_head[:, :, query_cols:]
    own_keys = all_kv[:, :kv_heads_all]
    own_values = all_kv[:, kv_heads_all:].astype(jnp.float32)
    scale = 1.0 / math.sqrt(head_dim)
    split_at = kv_heads_all * head_dim
    pre_keys = prefix_cache[:, :, :split_at].reshape(groups_dev, pre_local, kv_heads_all, head_dim)
    pre_values = prefix_cache[:, :, split_at:].reshape(
        groups_dev, pre_local, kv_heads_all, head_dim
    )
    suf_keys = suffix_cache[:, :, :split_at].reshape(requests, suf_local, kv_heads_all, head_dim)
    suf_values = suffix_cache[:, :, split_at:].reshape(requests, suf_local, kv_heads_all, head_dim)
    pre_scores = (
        jnp.einsum("rgqd,npgd->rgqnp", all_queries, pre_keys, preferred_element_type=jnp.float32)
        * scale
    )
    suf_scores = (
        jnp.einsum("rgqd,rsgd->rgqs", all_queries, suf_keys, preferred_element_type=jnp.float32)
        * scale
    )
    own_scores = (
        jnp.einsum("rgqd,rgd->rgq", all_queries, own_keys, preferred_element_type=jnp.float32)
        * scale
    )
    pre_slots = tensor_rank * pre_local + jnp.arange(pre_local)
    pre_valid = (member[:, :, None] & (pre_slots[None, None, :] < prefix_len[None, :, None]))[
        :, None, None, :, :
    ]
    suf_slots = tensor_rank * suf_local + jnp.arange(suf_local)
    suf_valid = (suf_slots[None, :] < suffix_len[:, None])[:, None, None, :]
    own_valid = tensor_rank == 0
    top_pre = jnp.max(jnp.where(pre_valid, pre_scores, NEGATIVE), axis=(3, 4))
    top_suf = jnp.max(jnp.where(suf_valid, suf_scores, NEGATIVE), axis=3)
    top_own = jnp.where(own_valid, own_scores, NEGATIVE)
    top_local = jnp.maximum(jnp.maximum(top_pre, top_suf), top_own)
    pre_weights = jnp.where(pre_valid, jnp.exp(pre_scores - top_local[..., None, None]), 0.0)
    suf_weights = jnp.where(suf_valid, jnp.exp(suf_scores - top_local[..., None]), 0.0)
    own_weights = jnp.where(own_valid, jnp.exp(own_scores - top_local), 0.0)
    total_local = jnp.sum(pre_weights, axis=(3, 4)) + jnp.sum(suf_weights, axis=3) + own_weights
    sums_local = jnp.einsum(
        "rgqnp,npgd->rgqd",
        pre_weights.astype(jnp.bfloat16),
        pre_values,
        preferred_element_type=jnp.float32,
    )
    sums_local = sums_local + jnp.einsum(
        "rgqs,rsgd->rgqd",
        suf_weights.astype(jnp.bfloat16),
        suf_values,
        preferred_element_type=jnp.float32,
    )
    own_low = own_weights.astype(jnp.bfloat16).astype(jnp.float32)
    sums_local = sums_local + own_low[..., None] * own_values[:, :, None, :]
    packed = jnp.concatenate(
        [
            sums_local.reshape(requests, heads_all, head_dim),
            top_local.reshape(requests, heads_all, 1),
            total_local.reshape(requests, heads_all, 1),
        ],
        axis=2,
    )
    packed = packed.reshape(requests, tensor_size, heads_here, head_dim + 2).transpose(1, 0, 2, 3)
    parts = lax.all_to_all(packed, "tensor", 0, 0, tiled=True)
    part_sums = parts[..., :head_dim]
    part_top = parts[..., head_dim]
    part_total = parts[..., head_dim + 1]
    top_all = jnp.max(part_top, axis=0)
    factor = jnp.exp(part_top - top_all[None])
    total_mine = jnp.sum(part_total * factor, axis=0)
    sums_mine = jnp.sum(part_sums * factor[..., None], axis=0)
    mixed = sums_mine / total_mine[..., None]
    attn_heads = mixed.reshape(requests, query_cols).astype(jnp.bfloat16)
    width_here = model_width // tensor_size
    tokens_here = residual_in.shape[0]
    attn_parts = lax.all_to_all(
        jnp.dot(attn_heads, out_weight, preferred_element_type=jnp.float32).astype(jnp.bfloat16),
        "tensor",
        split_axis=1,
        concat_axis=0,
        tiled=True,
    ).reshape(tensor_size, requests, width_here)
    attn_cols = jnp.sum(attn_parts.astype(jnp.float32), axis=0)
    residual_cols = lax.dynamic_slice_in_dim(residual_all, tensor_rank * width_here, width_here, 1)
    middle_cols = (residual_cols.astype(jnp.float32) + attn_cols).astype(jnp.bfloat16)
    middle_wide = middle_cols.astype(jnp.float32)
    square_sum = lax.psum(jnp.sum(middle_wide * middle_wide, axis=1, keepdims=True), "tensor")
    gain_cols = lax.dynamic_slice_in_dim(moe_gain, tensor_rank * width_here, width_here, 0)
    cols_in = (
        middle_wide * lax.rsqrt(square_sum / model_width + EPSILON) * gain_cols
    ).astype(jnp.bfloat16)
    local_experts = gate_weight.shape[0]
    experts_all = local_experts * owners
    topk = routes.shape[1]
    capacity = 2 * requests * topk // experts_all
    flat_routes = routes.reshape(-1)
    onehot = (flat_routes[:, None] == jnp.arange(experts_all)[None, :]).astype(jnp.int32)
    running = jnp.cumsum(onehot, axis=0)
    slot_of = jnp.sum(onehot * running, axis=1) - 1
    code_of = (flat_routes * capacity + slot_of).reshape(requests, topk)
    code_span = jnp.arange(experts_all * capacity)
    placing = jnp.any(code_of[None, :, :] == code_span[:, None, None], axis=2).astype(jnp.bfloat16)
    share = route_weights / jnp.sum(route_weights, axis=1, keepdims=True)
    placed = jnp.dot(placing, cols_in, preferred_element_type=jnp.float32)
    outgoing = placed.astype(jnp.bfloat16).reshape(owners, local_experts, capacity, width_here)
    chunks = 2 if local_experts % 2 == 0 else 1
    per_chunk = local_experts // chunks
    pieces = []
    for chunk in range(chunks):
        lo = chunk * per_chunk
        arrived = lax.all_to_all(
            outgoing[:, lo : lo + per_chunk], "dp", split_axis=0, concat_axis=0, tiled=True
        )
        rows = lax.all_gather(arrived, "tensor", axis=3, tiled=True)
        gate_val = jnp.einsum(
            "necd,edf->necf", rows, gate_weight[lo : lo + per_chunk], preferred_element_type=jnp.float32
        )
        lift_val = jnp.einsum(
            "necd,edf->necf", rows, lift_weight[lo : lo + per_chunk], preferred_element_type=jnp.float32
        )
        hidden_units = (jax.nn.silu(gate_val) * lift_val).astype(jnp.bfloat16)
        partial_out = jnp.einsum(
            "necf,efd->necd",
            hidden_units,
            down_weight[lo : lo + per_chunk],
            preferred_element_type=jnp.float32,
        ).astype(jnp.bfloat16)
        summed_out = lax.psum_scatter(partial_out, "tensor", scatter_dimension=3, tiled=True)
        pieces.append(
            lax.all_to_all(summed_out, "dp", split_axis=0, concat_axis=0, tiled=True)
        )
    returned = jnp.concatenate(pieces, axis=1).astype(jnp.float32)
    returned = returned.reshape(experts_all * capacity, width_here)
    picked_rows = returned[code_of]
    moe_cols = jnp.sum(share[:, :, None] * picked_rows, axis=1)
    layer_cols = (middle_wide + moe_cols).astype(jnp.bfloat16)
    layer_out = lax.all_to_all(layer_cols, "tensor", split_axis=0, concat_axis=1, tiled=True)
    return (layer_out, new_rows)


def solution(mesh):
    in_specs = (
        P(("dp", "tensor"), None),
        P(),
        P(None, "tensor"),
        P(None, "tensor"),
        P(),
        P(),
        P("tensor", None),
        P(),
        P("dp", None, "tensor"),
        P("dp", None, "tensor"),
        P("dp", "tensor", None),
        P("dp", None),
        P("dp", None),
        P("dp", "tensor", None),
        P("dp", "tensor", None),
        P("dp"),
        P("dp"),
        P("dp"),
    )
    out_specs = (P(("dp", "tensor"), None), P("dp", "tensor"))
    return jax.shard_map(body, mesh=mesh, in_specs=in_specs, out_specs=out_specs, check_vma=False)
```

```python
import math

import jax
import jax.numpy as jnp
from jax import lax
from jax.sharding import PartitionSpec as P

EPSILON = 1e-06
THETA = 1000000.0
NEGATIVE = -1e30


def rms_scale(values, gain):
    mean_square = jnp.mean(values * values, axis=-1, keepdims=True)
    return values * lax.rsqrt(mean_square + EPSILON) * gain


def rotate(values, positions):
    half = values.shape[-1] // 2
    freqs = THETA ** (-jnp.arange(half).astype(jnp.float32) * 2.0 / values.shape[-1])
    angles = positions.astype(jnp.float32)[:, None] * freqs[None, :]
    angles = jnp.concatenate([angles, angles], axis=-1)
    cosine = jnp.cos(angles)[:, None, :]
    sine = jnp.sin(angles)[:, None, :]
    turned = jnp.concatenate([-values[..., half:], values[..., :half]], axis=-1)
    return values * cosine + turned * sine


def body(
    residual_in,
    attn_gain,
    query_weight,
    kv_weight,
    query_gain,
    key_gain,
    out_weight,
    moe_gain,
    gate_weight,
    lift_weight,
    down_weight,
    routes,
    route_weights,
    prefix_cache,
    suffix_cache,
    prefix_len,
    suffix_len,
    request_group,
):
    tensor_size = lax.axis_size("tensor")
    tensor_rank = lax.axis_index("tensor")
    dp_rank = lax.axis_index("dp")
    owners = lax.axis_size("dp")
    head_dim = query_gain.shape[0]
    requests = routes.shape[0]
    model_width = residual_in.shape[1]
    query_cols = query_weight.shape[1]
    kv_cols = kv_weight.shape[1]
    heads_here = query_cols // head_dim
    heads_all = heads_here * tensor_size
    kv_heads_all = kv_cols * tensor_size // (2 * head_dim)
    per_group = heads_all // kv_heads_all
    groups_dev = prefix_cache.shape[0]
    pre_local = prefix_cache.shape[1]
    suf_local = suffix_cache.shape[1]
    residual_all = lax.all_gather(residual_in, "tensor", axis=0, tiled=True)
    piece = rms_scale(residual_all.astype(jnp.float32), attn_gain).astype(jnp.bfloat16)
    projected = jnp.concatenate(
        [
            jnp.dot(piece, query_weight, preferred_element_type=jnp.float32),
            jnp.dot(piece, kv_weight, preferred_element_type=jnp.float32),
        ],
        axis=1,
    )
    query_raw = projected[:, :query_cols].reshape(requests, heads_here, head_dim)
    kv_raw = projected[:, query_cols:].reshape(requests, kv_cols // head_dim, head_dim)
    group_ids = dp_rank * groups_dev + jnp.arange(groups_dev)
    member = request_group[:, None] == group_ids[None, :]
    prefix_of = jnp.sum(jnp.where(member, prefix_len[None, :], 0), axis=1)
    positions = prefix_of + suffix_len
    queries = rotate(rms_scale(query_raw, query_gain), positions).astype(jnp.bfloat16)
    head_number = tensor_rank * (kv_cols // head_dim) + jnp.arange(kv_cols // head_dim)
    is_key = (head_number < kv_heads_all)[None, :, None]
    keyed = rotate(rms_scale(kv_raw, key_gain), positions)
    new_rows = jnp.where(is_key, keyed, kv_raw).astype(jnp.bfloat16).reshape(requests, kv_cols)
    joined = jnp.concatenate([queries.reshape(requests, query_cols), new_rows], axis=1)
    every_head = lax.all_gather(joined, "tensor", axis=1, tiled=True).reshape(
        requests, tensor_size, query_cols + kv_cols
    )
    all_queries = every_head[:, :, :query_cols].reshape(requests, kv_heads_all, per_group, head_dim)
    all_kv = every_head[:, :, query_cols:]
    own_keys = all_kv[:, :kv_heads_all]
    own_values = all_kv[:, kv_heads_all:].astype(jnp.float32)
    scale = 1.0 / math.sqrt(head_dim)
    split_at = kv_heads_all * head_dim
    pre_keys = prefix_cache[:, :, :split_at].reshape(groups_dev, pre_local, kv_heads_all, head_dim)
    pre_values = prefix_cache[:, :, split_at:].reshape(
        groups_dev, pre_local, kv_heads_all, head_dim
    )
    suf_keys = suffix_cache[:, :, :split_at].reshape(requests, suf_local, kv_heads_all, head_dim)
    suf_values = suffix_cache[:, :, split_at:].reshape(requests, suf_local, kv_heads_all, head_dim)
    pre_scores = (
        jnp.einsum("rgqd,npgd->rgqnp", all_queries, pre_keys, preferred_element_type=jnp.float32)
        * scale
    )
    suf_scores = (
        jnp.einsum("rgqd,rsgd->rgqs", all_queries, suf_keys, preferred_element_type=jnp.float32)
        * scale
    )
    own_scores = (
        jnp.einsum("rgqd,rgd->rgq", all_queries, own_keys, preferred_element_type=jnp.float32)
        * scale
    )
    pre_slots = tensor_rank * pre_local + jnp.arange(pre_local)
    pre_valid = (member[:, :, None] & (pre_slots[None, None, :] < prefix_len[None, :, None]))[
        :, None, None, :, :
    ]
    suf_slots = tensor_rank * suf_local + jnp.arange(suf_local)
    suf_valid = (suf_slots[None, :] < suffix_len[:, None])[:, None, None, :]
    own_valid = tensor_rank == 0
    top_pre = jnp.max(jnp.where(pre_valid, pre_scores, NEGATIVE), axis=(3, 4))
    top_suf = jnp.max(jnp.where(suf_valid, suf_scores, NEGATIVE), axis=3)
    top_own = jnp.where(own_valid, own_scores, NEGATIVE)
    top_local = jnp.maximum(jnp.maximum(top_pre, top_suf), top_own)
    pre_weights = jnp.where(pre_valid, jnp.exp(pre_scores - top_local[..., None, None]), 0.0)
    suf_weights = jnp.where(suf_valid, jnp.exp(suf_scores - top_local[..., None]), 0.0)
    own_weights = jnp.where(own_valid, jnp.exp(own_scores - top_local), 0.0)
    total_local = jnp.sum(pre_weights, axis=(3, 4)) + jnp.sum(suf_weights, axis=3) + own_weights
    sums_local = jnp.einsum(
        "rgqnp,npgd->rgqd",
        pre_weights.astype(jnp.bfloat16),
        pre_values,
        preferred_element_type=jnp.float32,
    )
    sums_local = sums_local + jnp.einsum(
        "rgqs,rsgd->rgqd",
        suf_weights.astype(jnp.bfloat16),
        suf_values,
        preferred_element_type=jnp.float32,
    )
    own_low = own_weights.astype(jnp.bfloat16).astype(jnp.float32)
    sums_local = sums_local + own_low[..., None] * own_values[:, :, None, :]
    pair_rows = requests * heads_here // head_dim

    def by_owner(values):
        values = values.reshape(requests, tensor_size, heads_here, -1).transpose(1, 0, 2, 3)
        return values.reshape(tensor_size, -1, head_dim)

    packed = jnp.concatenate(
        [by_owner(sums_local), by_owner(top_local), by_owner(total_local)], axis=1
    )
    parts = lax.all_to_all(packed, "tensor", 0, 0, tiled=True)
    spread = requests * heads_here
    part_sums = parts[:, :spread].reshape(tensor_size, requests, heads_here, head_dim)
    part_top = parts[:, spread : spread + pair_rows].reshape(tensor_size, requests, heads_here)
    part_total = parts[:, spread + pair_rows :].reshape(tensor_size, requests, heads_here)
    top_all = jnp.max(part_top, axis=0)
    factor = jnp.exp(part_top - top_all[None])
    total_mine = jnp.sum(part_total * factor, axis=0)
    sums_mine = jnp.sum(part_sums * factor[..., None], axis=0)
    mixed = sums_mine / total_mine[..., None]
    attn_heads = mixed.reshape(requests, query_cols).astype(jnp.bfloat16)
    width_here = model_width // tensor_size
    tokens_here = residual_in.shape[0]
    attn_parts = lax.all_to_all(
        jnp.dot(attn_heads, out_weight, preferred_element_type=jnp.float32).astype(jnp.bfloat16),
        "tensor",
        split_axis=1,
        concat_axis=0,
        tiled=True,
    ).reshape(tensor_size, requests, width_here)
    attn_cols = jnp.sum(attn_parts.astype(jnp.float32), axis=0)
    residual_cols = lax.dynamic_slice_in_dim(residual_all, tensor_rank * width_here, width_here, 1)
    middle_cols = (residual_cols.astype(jnp.float32) + attn_cols).astype(jnp.bfloat16)
    middle_wide = middle_cols.astype(jnp.float32)
    square_sum = lax.psum(jnp.sum(middle_wide * middle_wide, axis=1, keepdims=True), "tensor")
    gain_cols = lax.dynamic_slice_in_dim(moe_gain, tensor_rank * width_here, width_here, 0)
    cols_in = (
        middle_wide * lax.rsqrt(square_sum / model_width + EPSILON) * gain_cols
    ).astype(jnp.bfloat16)
    local_experts = gate_weight.shape[0]
    experts_all = local_experts * owners
    topk = routes.shape[1]
    capacity = 2 * requests * topk // experts_all
    flat_routes = routes.reshape(-1)
    onehot = (flat_routes[:, None] == jnp.arange(experts_all)[None, :]).astype(jnp.int32)
    running = jnp.cumsum(onehot, axis=0)
    slot_of = jnp.sum(onehot * running, axis=1) - 1
    code_of = (flat_routes * capacity + slot_of).reshape(requests, topk)
    code_span = jnp.arange(experts_all * capacity)
    placing = jnp.any(code_of[None, :, :] == code_span[:, None, None], axis=2).astype(jnp.bfloat16)
    share = route_weights / jnp.sum(route_weights, axis=1, keepdims=True)
    placed = jnp.dot(placing, cols_in, preferred_element_type=jnp.float32)
    outgoing = placed.astype(jnp.bfloat16).reshape(owners, local_experts * capacity, width_here)
    arrived = lax.all_to_all(outgoing, "dp", split_axis=0, concat_axis=0, tiled=True)
    rows = lax.all_gather(arrived, "tensor", axis=2, tiled=True).reshape(
        owners, local_experts, capacity, model_width
    )
    gate_val = jnp.einsum("necd,edf->necf", rows, gate_weight, preferred_element_type=jnp.float32)
    lift_val = jnp.einsum("necd,edf->necf", rows, lift_weight, preferred_element_type=jnp.float32)
    hidden_units = (jax.nn.silu(gate_val) * lift_val).astype(jnp.bfloat16)
    partial_out = jnp.einsum(
        "necf,efd->necd", hidden_units, down_weight, preferred_element_type=jnp.float32
    ).astype(jnp.bfloat16)
    summed_out = lax.psum_scatter(partial_out, "tensor", scatter_dimension=3, tiled=True)
    returned = lax.all_to_all(
        summed_out.reshape(owners, local_experts * capacity, width_here),
        "dp",
        split_axis=0,
        concat_axis=0,
        tiled=True,
    ).astype(jnp.float32)
    returned = returned.reshape(experts_all * capacity, width_here)
    picked_rows = returned[code_of]
    moe_cols = jnp.sum(share[:, :, None] * picked_rows, axis=1)
    layer_cols = (middle_wide + moe_cols).astype(jnp.bfloat16)
    layer_out = lax.all_to_all(layer_cols, "tensor", split_axis=0, concat_axis=1, tiled=True)
    return (layer_out, new_rows)


def solution(mesh):
    in_specs = (
        P(("dp", "tensor"), None),
        P(),
        P(None, "tensor"),
        P(None, "tensor"),
        P(),
        P(),
        P("tensor", None),
        P(),
        P("dp", None, "tensor"),
        P("dp", None, "tensor"),
        P("dp", "tensor", None),
        P("dp", None),
        P("dp", None),
        P("dp", "tensor", None),
        P("dp", "tensor", None),
        P("dp"),
        P("dp"),
        P("dp"),
    )
    out_specs = (P(("dp", "tensor"), None), P("dp", "tensor"))
    return jax.shard_map(body, mesh=mesh, in_specs=in_specs, out_specs=out_specs, check_vma=False)
```

```python
import math

import jax
import jax.numpy as jnp
from jax import lax
from jax.sharding import PartitionSpec as P

EPSILON = 1e-06
THETA = 1000000.0
NEGATIVE = -1e30


def rms_scale(values, gain):
    mean_square = jnp.mean(values * values, axis=-1, keepdims=True)
    return values * lax.rsqrt(mean_square + EPSILON) * gain


def rotate(values, positions):
    half = values.shape[-1] // 2
    freqs = THETA ** (-jnp.arange(half).astype(jnp.float32) * 2.0 / values.shape[-1])
    angles = positions.astype(jnp.float32)[:, None] * freqs[None, :]
    angles = jnp.concatenate([angles, angles], axis=-1)
    cosine = jnp.cos(angles)[:, None, :]
    sine = jnp.sin(angles)[:, None, :]
    turned = jnp.concatenate([-values[..., half:], values[..., :half]], axis=-1)
    return values * cosine + turned * sine


def body(
    residual_in,
    attn_gain,
    query_weight,
    kv_weight,
    query_gain,
    key_gain,
    out_weight,
    moe_gain,
    gate_weight,
    lift_weight,
    down_weight,
    routes,
    route_weights,
    prefix_cache,
    suffix_cache,
    prefix_len,
    suffix_len,
    request_group,
):
    tensor_size = lax.axis_size("tensor")
    tensor_rank = lax.axis_index("tensor")
    dp_rank = lax.axis_index("dp")
    owners = lax.axis_size("dp")
    head_dim = query_gain.shape[0]
    requests = routes.shape[0]
    model_width = residual_in.shape[1]
    query_cols = query_weight.shape[1]
    kv_cols = kv_weight.shape[1]
    heads_here = query_cols // head_dim
    heads_all = heads_here * tensor_size
    kv_heads_all = kv_cols * tensor_size // (2 * head_dim)
    per_group = heads_all // kv_heads_all
    groups_dev = prefix_cache.shape[0]
    pre_local = prefix_cache.shape[1]
    suf_local = suffix_cache.shape[1]
    residual_all = lax.all_gather(residual_in, "tensor", axis=0, tiled=True)
    piece = rms_scale(residual_all.astype(jnp.float32), attn_gain).astype(jnp.bfloat16)
    projected = jnp.concatenate(
        [
            jnp.dot(piece, query_weight, preferred_element_type=jnp.float32),
            jnp.dot(piece, kv_weight, preferred_element_type=jnp.float32),
        ],
        axis=1,
    )
    query_raw = projected[:, :query_cols].reshape(requests, heads_here, head_dim)
    kv_raw = projected[:, query_cols:].reshape(requests, kv_cols // head_dim, head_dim)
    group_ids = dp_rank * groups_dev + jnp.arange(groups_dev)
    member = request_group[:, None] == group_ids[None, :]
    prefix_of = jnp.sum(jnp.where(member, prefix_len[None, :], 0), axis=1)
    positions = prefix_of + suffix_len
    queries = rotate(rms_scale(query_raw, query_gain), positions).astype(jnp.bfloat16)
    head_number = tensor_rank * (kv_cols // head_dim) + jnp.arange(kv_cols // head_dim)
    is_key = (head_number < kv_heads_all)[None, :, None]
    keyed = rotate(rms_scale(kv_raw, key_gain), positions)
    new_rows = jnp.where(is_key, keyed, kv_raw).astype(jnp.bfloat16).reshape(requests, kv_cols)
    joined = jnp.concatenate([queries.reshape(requests, query_cols), new_rows], axis=1)
    every_head = lax.all_gather(joined, "tensor", axis=1, tiled=True).reshape(
        requests, tensor_size, query_cols + kv_cols
    )
    all_queries = every_head[:, :, :query_cols].reshape(requests, kv_heads_all, per_group, head_dim)
    all_kv = every_head[:, :, query_cols:]
    own_keys = all_kv[:, :kv_heads_all]
    own_values = all_kv[:, kv_heads_all:].astype(jnp.float32)
    scale = 1.0 / math.sqrt(head_dim)
    split_at = kv_heads_all * head_dim
    pre_keys = prefix_cache[:, :, :split_at].reshape(groups_dev, pre_local, kv_heads_all, head_dim)
    pre_values = prefix_cache[:, :, split_at:].reshape(
        groups_dev, pre_local, kv_heads_all, head_dim
    )
    suf_keys = suffix_cache[:, :, :split_at].reshape(requests, suf_local, kv_heads_all, head_dim)
    suf_values = suffix_cache[:, :, split_at:].reshape(requests, suf_local, kv_heads_all, head_dim)
    pre_scores = (
        jnp.einsum("rgqd,npgd->rgqnp", all_queries, pre_keys, preferred_element_type=jnp.float32)
        * scale
    )
    suf_scores = (
        jnp.einsum("rgqd,rsgd->rgqs", all_queries, suf_keys, preferred_element_type=jnp.float32)
        * scale
    )
    own_scores = (
        jnp.einsum("rgqd,rgd->rgq", all_queries, own_keys, preferred_element_type=jnp.float32)
        * scale
    )
    pre_slots = tensor_rank * pre_local + jnp.arange(pre_local)
    pre_valid = (member[:, :, None] & (pre_slots[None, None, :] < prefix_len[None, :, None]))[
        :, None, None, :, :
    ]
    suf_slots = tensor_rank * suf_local + jnp.arange(suf_local)
    suf_valid = (suf_slots[None, :] < suffix_len[:, None])[:, None, None, :]
    own_valid = tensor_rank == 0
    top_pre = jnp.max(jnp.where(pre_valid, pre_scores, NEGATIVE), axis=(3, 4))
    top_suf = jnp.max(jnp.where(suf_valid, suf_scores, NEGATIVE), axis=3)
    top_own = jnp.where(own_valid, own_scores, NEGATIVE)
    top_local = jnp.maximum(jnp.maximum(top_pre, top_suf), top_own)
    pre_weights = jnp.where(pre_valid, jnp.exp(pre_scores - top_local[..., None, None]), 0.0)
    suf_weights = jnp.where(suf_valid, jnp.exp(suf_scores - top_local[..., None]), 0.0)
    own_weights = jnp.where(own_valid, jnp.exp(own_scores - top_local), 0.0)
    total_local = jnp.sum(pre_weights, axis=(3, 4)) + jnp.sum(suf_weights, axis=3) + own_weights
    sums_local = jnp.einsum(
        "rgqnp,npgd->rgqd",
        pre_weights.astype(jnp.bfloat16),
        pre_values,
        preferred_element_type=jnp.float32,
    )
    sums_local = sums_local + jnp.einsum(
        "rgqs,rsgd->rgqd",
        suf_weights.astype(jnp.bfloat16),
        suf_values,
        preferred_element_type=jnp.float32,
    )
    own_low = own_weights.astype(jnp.bfloat16).astype(jnp.float32)
    sums_local = sums_local + own_low[..., None] * own_values[:, :, None, :]
    pair_rows = requests * heads_here // head_dim

    def by_owner(values):
        values = values.reshape(requests, tensor_size, heads_here, -1).transpose(1, 0, 2, 3)
        return values.reshape(tensor_size, -1, head_dim)

    packed = jnp.concatenate(
        [by_owner(sums_local), by_owner(top_local), by_owner(total_local)], axis=1
    )
    parts = lax.all_to_all(packed, "tensor", 0, 0, tiled=True)
    spread = requests * heads_here
    part_sums = parts[:, :spread].reshape(tensor_size, requests, heads_here, head_dim)
    part_top = parts[:, spread : spread + pair_rows].reshape(tensor_size, requests, heads_here)
    part_total = parts[:, spread + pair_rows :].reshape(tensor_size, requests, heads_here)
    top_all = jnp.max(part_top, axis=0)
    factor = jnp.exp(part_top - top_all[None])
    total_mine = jnp.sum(part_total * factor, axis=0)
    sums_mine = jnp.sum(part_sums * factor[..., None], axis=0)
    mixed = sums_mine / total_mine[..., None]
    attn_heads = mixed.reshape(requests, query_cols).astype(jnp.bfloat16)
    width_here = model_width // tensor_size
    tokens_here = residual_in.shape[0]
    attn_parts = lax.all_to_all(
        jnp.dot(attn_heads, out_weight, preferred_element_type=jnp.float32).astype(jnp.bfloat16),
        "tensor",
        split_axis=1,
        concat_axis=0,
        tiled=True,
    ).reshape(tensor_size, requests, width_here)
    attn_cols = jnp.sum(attn_parts.astype(jnp.float32), axis=0)
    residual_cols = lax.dynamic_slice_in_dim(residual_all, tensor_rank * width_here, width_here, 1)
    middle_cols = (residual_cols.astype(jnp.float32) + attn_cols).astype(jnp.bfloat16)
    middle_wide = middle_cols.astype(jnp.float32)
    square_sum = lax.psum(jnp.sum(middle_wide * middle_wide, axis=1, keepdims=True), "tensor")
    gain_cols = lax.dynamic_slice_in_dim(moe_gain, tensor_rank * width_here, width_here, 0)
    cols_in = (
        middle_wide * lax.rsqrt(square_sum / model_width + EPSILON) * gain_cols
    ).astype(jnp.bfloat16)
    local_experts = gate_weight.shape[0]
    experts_all = local_experts * owners
    topk = routes.shape[1]
    capacity = 2 * requests * topk // experts_all
    flat_routes = routes.reshape(-1)
    onehot = (flat_routes[:, None] == jnp.arange(experts_all)[None, :]).astype(jnp.int32)
    running = jnp.cumsum(onehot, axis=0)
    slot_of = jnp.sum(onehot * running, axis=1) - 1
    code_of = (flat_routes * capacity + slot_of).reshape(requests, topk)
    code_span = jnp.arange(experts_all * capacity)
    placing = jnp.any(code_of[None, :, :] == code_span[:, None, None], axis=2).astype(jnp.bfloat16)
    share = route_weights / jnp.sum(route_weights, axis=1, keepdims=True)
    placed = jnp.dot(placing, cols_in, preferred_element_type=jnp.float32)
    outgoing = placed.astype(jnp.bfloat16).reshape(owners, local_experts * capacity, width_here)
    arrived = lax.all_to_all(outgoing, "dp", split_axis=0, concat_axis=0, tiled=True)
    rows = lax.all_gather(arrived, "tensor", axis=2, tiled=True).reshape(
        owners, local_experts, capacity, model_width
    )
    gate_val = jnp.einsum("necd,edf->necf", rows, gate_weight, preferred_element_type=jnp.float32)
    lift_val = jnp.einsum("necd,edf->necf", rows, lift_weight, preferred_element_type=jnp.float32)
    hidden_units = (jax.nn.silu(gate_val) * lift_val).astype(jnp.bfloat16)
    hidden_all = lax.all_gather(hidden_units, "tensor", axis=3, tiled=True)
    down_cols = lax.all_to_all(down_weight, "tensor", split_axis=2, concat_axis=1, tiled=True)
    summed_out = jnp.einsum(
        "necf,efd->necd", hidden_all, down_cols, preferred_element_type=jnp.float32
    ).astype(jnp.bfloat16)
    returned = lax.all_to_all(
        summed_out.reshape(owners, local_experts * capacity, width_here),
        "dp",
        split_axis=0,
        concat_axis=0,
        tiled=True,
    ).astype(jnp.float32)
    returned = returned.reshape(experts_all * capacity, width_here)
    picked_rows = returned[code_of]
    moe_cols = jnp.sum(share[:, :, None] * picked_rows, axis=1)
    layer_cols = (middle_wide + moe_cols).astype(jnp.bfloat16)
    layer_out = lax.all_to_all(layer_cols, "tensor", split_axis=0, concat_axis=1, tiled=True)
    return (layer_out, new_rows)


def solution(mesh):
    in_specs = (
        P(("dp", "tensor"), None),
        P(),
        P(None, "tensor"),
        P(None, "tensor"),
        P(),
        P(),
        P("tensor", None),
        P(),
        P("dp", None, "tensor"),
        P("dp", None, "tensor"),
        P("dp", "tensor", None),
        P("dp", None),
        P("dp", None),
        P("dp", "tensor", None),
        P("dp", "tensor", None),
        P("dp"),
        P("dp"),
        P("dp"),
    )
    out_specs = (P(("dp", "tensor"), None), P("dp", "tensor"))
    return jax.shard_map(body, mesh=mesh, in_specs=in_specs, out_specs=out_specs, check_vma=False)
```

```python
import math

import jax
import jax.numpy as jnp
from jax import lax
from jax.sharding import PartitionSpec as P

EPSILON = 1e-06
THETA = 1000000.0
NEGATIVE = -1e30


def rms_scale(values, gain):
    mean_square = jnp.mean(values * values, axis=-1, keepdims=True)
    return values * lax.rsqrt(mean_square + EPSILON) * gain


def rotate(values, positions):
    half = values.shape[-1] // 2
    freqs = THETA ** (-jnp.arange(half).astype(jnp.float32) * 2.0 / values.shape[-1])
    angles = positions.astype(jnp.float32)[:, None] * freqs[None, :]
    angles = jnp.concatenate([angles, angles], axis=-1)
    cosine = jnp.cos(angles)[:, None, :]
    sine = jnp.sin(angles)[:, None, :]
    turned = jnp.concatenate([-values[..., half:], values[..., :half]], axis=-1)
    return values * cosine + turned * sine


def body(
    residual_in,
    attn_gain,
    query_weight,
    kv_weight,
    query_gain,
    key_gain,
    out_weight,
    moe_gain,
    gate_weight,
    lift_weight,
    down_weight,
    routes,
    route_weights,
    prefix_cache,
    suffix_cache,
    prefix_len,
    suffix_len,
    request_group,
):
    tensor_size = lax.axis_size("tensor")
    tensor_rank = lax.axis_index("tensor")
    dp_rank = lax.axis_index("dp")
    owners = lax.axis_size("dp")
    head_dim = query_gain.shape[0]
    requests = routes.shape[0]
    model_width = residual_in.shape[1]
    query_cols = query_weight.shape[1]
    kv_cols = kv_weight.shape[1]
    heads_here = query_cols // head_dim
    heads_all = heads_here * tensor_size
    kv_heads_all = kv_cols * tensor_size // (2 * head_dim)
    per_group = heads_all // kv_heads_all
    groups_dev = prefix_cache.shape[0]
    pre_local = prefix_cache.shape[1]
    suf_local = suffix_cache.shape[1]
    residual_all = lax.all_gather(residual_in, "tensor", axis=0, tiled=True)
    piece = rms_scale(residual_all.astype(jnp.float32), attn_gain).astype(jnp.bfloat16)
    projected = jnp.concatenate(
        [
            jnp.dot(piece, query_weight, preferred_element_type=jnp.float32),
            jnp.dot(piece, kv_weight, preferred_element_type=jnp.float32),
        ],
        axis=1,
    )
    query_raw = projected[:, :query_cols].reshape(requests, heads_here, head_dim)
    kv_raw = projected[:, query_cols:].reshape(requests, kv_cols // head_dim, head_dim)
    group_ids = dp_rank * groups_dev + jnp.arange(groups_dev)
    member = request_group[:, None] == group_ids[None, :]
    prefix_of = jnp.sum(jnp.where(member, prefix_len[None, :], 0), axis=1)
    positions = prefix_of + suffix_len
    queries = rotate(rms_scale(query_raw, query_gain), positions).astype(jnp.bfloat16)
    head_number = tensor_rank * (kv_cols // head_dim) + jnp.arange(kv_cols // head_dim)
    is_key = (head_number < kv_heads_all)[None, :, None]
    keyed = rotate(rms_scale(kv_raw, key_gain), positions)
    new_rows = jnp.where(is_key, keyed, kv_raw).astype(jnp.bfloat16).reshape(requests, kv_cols)
    joined = jnp.concatenate([queries.reshape(requests, query_cols), new_rows], axis=1)
    every_head = lax.all_gather(joined, "tensor", axis=1, tiled=True).reshape(
        requests, tensor_size, query_cols + kv_cols
    )
    all_queries = every_head[:, :, :query_cols].reshape(requests, kv_heads_all, per_group, head_dim)
    all_kv = every_head[:, :, query_cols:]
    own_keys = all_kv[:, :kv_heads_all]
    own_values = all_kv[:, kv_heads_all:].astype(jnp.float32)
    scale = 1.0 / math.sqrt(head_dim)
    split_at = kv_heads_all * head_dim
    pre_keys = prefix_cache[:, :, :split_at].reshape(groups_dev, pre_local, kv_heads_all, head_dim)
    pre_values = prefix_cache[:, :, split_at:].reshape(
        groups_dev, pre_local, kv_heads_all, head_dim
    )
    suf_keys = suffix_cache[:, :, :split_at].reshape(requests, suf_local, kv_heads_all, head_dim)
    suf_values = suffix_cache[:, :, split_at:].reshape(requests, suf_local, kv_heads_all, head_dim)
    pre_scores = (
        jnp.einsum("rgqd,npgd->rgqnp", all_queries, pre_keys, preferred_element_type=jnp.float32)
        * scale
    )
    suf_scores = (
        jnp.einsum("rgqd,rsgd->rgqs", all_queries, suf_keys, preferred_element_type=jnp.float32)
        * scale
    )
    own_scores = (
        jnp.einsum("rgqd,rgd->rgq", all_queries, own_keys, preferred_element_type=jnp.float32)
        * scale
    )
    pre_slots = tensor_rank * pre_local + jnp.arange(pre_local)
    pre_valid = (member[:, :, None] & (pre_slots[None, None, :] < prefix_len[None, :, None]))[
        :, None, None, :, :
    ]
    suf_slots = tensor_rank * suf_local + jnp.arange(suf_local)
    suf_valid = (suf_slots[None, :] < suffix_len[:, None])[:, None, None, :]
    own_valid = tensor_rank == 0
    top_pre = jnp.max(jnp.where(pre_valid, pre_scores, NEGATIVE), axis=(3, 4))
    top_suf = jnp.max(jnp.where(suf_valid, suf_scores, NEGATIVE), axis=3)
    top_own = jnp.where(own_valid, own_scores, NEGATIVE)
    top_local = (
        jnp.maximum(jnp.maximum(top_pre, top_suf), top_own).astype(jnp.bfloat16).astype(jnp.float32)
    )
    pre_weights = jnp.where(pre_valid, jnp.exp(pre_scores - top_local[..., None, None]), 0.0)
    suf_weights = jnp.where(suf_valid, jnp.exp(suf_scores - top_local[..., None]), 0.0)
    own_weights = jnp.where(own_valid, jnp.exp(own_scores - top_local), 0.0)
    total_local = jnp.sum(pre_weights, axis=(3, 4)) + jnp.sum(suf_weights, axis=3) + own_weights
    sums_local = jnp.einsum(
        "rgqnp,npgd->rgqd",
        pre_weights.astype(jnp.bfloat16),
        pre_values,
        preferred_element_type=jnp.float32,
    )
    sums_local = sums_local + jnp.einsum(
        "rgqs,rsgd->rgqd",
        suf_weights.astype(jnp.bfloat16),
        suf_values,
        preferred_element_type=jnp.float32,
    )
    own_low = own_weights.astype(jnp.bfloat16).astype(jnp.float32)
    sums_local = sums_local + own_low[..., None] * own_values[:, :, None, :]
    pair_rows = requests * heads_here // head_dim

    def by_owner(values):
        values = values.reshape(requests, tensor_size, heads_here, -1).transpose(1, 0, 2, 3)
        return values.reshape(tensor_size, -1, head_dim)

    total_high = total_local.astype(jnp.bfloat16)
    total_low = (total_local - total_high.astype(jnp.float32)).astype(jnp.bfloat16)
    packed = jnp.concatenate(
        [
            by_owner(sums_local.astype(jnp.bfloat16)),
            by_owner(top_local.astype(jnp.bfloat16)),
            by_owner(total_high),
            by_owner(total_low),
        ],
        axis=1,
    )
    parts = lax.all_to_all(packed, "tensor", 0, 0, tiled=True).astype(jnp.float32)
    spread = requests * heads_here
    part_sums = parts[:, :spread].reshape(tensor_size, requests, heads_here, head_dim)
    part_top = parts[:, spread : spread + pair_rows].reshape(tensor_size, requests, heads_here)
    part_total = (
        parts[:, spread + pair_rows : spread + 2 * pair_rows]
        + parts[:, spread + 2 * pair_rows :]
    ).reshape(tensor_size, requests, heads_here)
    top_all = jnp.max(part_top, axis=0)
    factor = jnp.exp(part_top - top_all[None])
    total_mine = jnp.sum(part_total * factor, axis=0)
    sums_mine = jnp.sum(part_sums * factor[..., None], axis=0)
    mixed = sums_mine / total_mine[..., None]
    attn_heads = mixed.reshape(requests, query_cols).astype(jnp.bfloat16)
    width_here = model_width // tensor_size
    tokens_here = residual_in.shape[0]
    attn_parts = lax.all_to_all(
        jnp.dot(attn_heads, out_weight, preferred_element_type=jnp.float32).astype(jnp.bfloat16),
        "tensor",
        split_axis=0,
        concat_axis=0,
        tiled=True,
    ).reshape(tensor_size, tokens_here, model_width)
    attn_out = jnp.sum(attn_parts.astype(jnp.float32), axis=0)
    middle = (residual_in.astype(jnp.float32) + attn_out).astype(jnp.bfloat16)
    moe_in = rms_scale(middle.astype(jnp.float32), moe_gain).astype(jnp.bfloat16)
    cols_in = lax.all_to_all(moe_in, "tensor", split_axis=1, concat_axis=0, tiled=True)
    local_experts = gate_weight.shape[0]
    experts_all = local_experts * owners
    topk = routes.shape[1]
    capacity = 2 * requests * topk // experts_all
    flat_routes = routes.reshape(-1)
    onehot = (flat_routes[:, None] == jnp.arange(experts_all)[None, :]).astype(jnp.int32)
    running = jnp.cumsum(onehot, axis=0)
    slot_of = jnp.sum(onehot * running, axis=1) - 1
    code_of = (flat_routes * capacity + slot_of).reshape(requests, topk)
    code_span = jnp.arange(experts_all * capacity)
    placing = jnp.any(code_of[None, :, :] == code_span[:, None, None], axis=2).astype(jnp.bfloat16)
    share = route_weights / jnp.sum(route_weights, axis=1, keepdims=True)
    placed = jnp.dot(placing, cols_in, preferred_element_type=jnp.float32)
    outgoing = placed.astype(jnp.bfloat16).reshape(owners, local_experts * capacity, width_here)
    arrived = lax.all_to_all(outgoing, "dp", split_axis=0, concat_axis=0, tiled=True)
    rows = lax.all_gather(arrived, "tensor", axis=2, tiled=True).reshape(
        owners, local_experts, capacity, model_width
    )
    gate_val = jnp.einsum("necd,edf->necf", rows, gate_weight, preferred_element_type=jnp.float32)
    lift_val = jnp.einsum("necd,edf->necf", rows, lift_weight, preferred_element_type=jnp.float32)
    hidden_units = (jax.nn.silu(gate_val) * lift_val).astype(jnp.bfloat16)
    partial_out = jnp.einsum(
        "necf,efd->necd", hidden_units, down_weight, preferred_element_type=jnp.float32
    ).astype(jnp.bfloat16)
    summed_out = lax.psum_scatter(partial_out, "tensor", scatter_dimension=3, tiled=True)
    returned = lax.all_to_all(
        summed_out.reshape(owners, local_experts * capacity, width_here),
        "dp",
        split_axis=0,
        concat_axis=0,
        tiled=True,
    ).astype(jnp.float32)
    returned = returned.reshape(experts_all * capacity, width_here)
    picked_rows = returned[code_of]
    moe_cols = jnp.sum(share[:, :, None] * picked_rows, axis=1).astype(jnp.bfloat16)
    moe_out = lax.all_to_all(moe_cols, "tensor", split_axis=0, concat_axis=1, tiled=True)
    layer_out = (middle.astype(jnp.float32) + moe_out.astype(jnp.float32)).astype(jnp.bfloat16)
    return (layer_out, new_rows)


def solution(mesh):
    in_specs = (
        P(("dp", "tensor"), None),
        P(),
        P(None, "tensor"),
        P(None, "tensor"),
        P(),
        P(),
        P("tensor", None),
        P(),
        P("dp", None, "tensor"),
        P("dp", None, "tensor"),
        P("dp", "tensor", None),
        P("dp", None),
        P("dp", None),
        P("dp", "tensor", None),
        P("dp", "tensor", None),
        P("dp"),
        P("dp"),
        P("dp"),
    )
    out_specs = (P(("dp", "tensor"), None), P("dp", "tensor"))
    return jax.shard_map(body, mesh=mesh, in_specs=in_specs, out_specs=out_specs, check_vma=False)
```

```python
import math

import jax
import jax.numpy as jnp
from jax import lax
from jax.sharding import PartitionSpec as P

EPSILON = 1e-06
THETA = 1000000.0
NEGATIVE = -1e30


def rms_scale(values, gain):
    mean_square = jnp.mean(values * values, axis=-1, keepdims=True)
    return values * lax.rsqrt(mean_square + EPSILON) * gain


def rotate(values, positions):
    half = values.shape[-1] // 2
    freqs = THETA ** (-jnp.arange(half).astype(jnp.float32) * 2.0 / values.shape[-1])
    angles = positions.astype(jnp.float32)[:, None] * freqs[None, :]
    angles = jnp.concatenate([angles, angles], axis=-1)
    cosine = jnp.cos(angles)[:, None, :]
    sine = jnp.sin(angles)[:, None, :]
    turned = jnp.concatenate([-values[..., half:], values[..., :half]], axis=-1)
    return values * cosine + turned * sine


def body(
    residual_in,
    attn_gain,
    query_weight,
    kv_weight,
    query_gain,
    key_gain,
    out_weight,
    moe_gain,
    gate_weight,
    lift_weight,
    down_weight,
    routes,
    route_weights,
    prefix_cache,
    suffix_cache,
    prefix_len,
    suffix_len,
    request_group,
):
    tensor_size = lax.axis_size("tensor")
    tensor_rank = lax.axis_index("tensor")
    dp_rank = lax.axis_index("dp")
    owners = lax.axis_size("dp")
    head_dim = query_gain.shape[0]
    requests = routes.shape[0]
    model_width = residual_in.shape[1]
    query_cols = query_weight.shape[1]
    kv_cols = kv_weight.shape[1]
    heads_here = query_cols // head_dim
    heads_all = heads_here * tensor_size
    kv_heads_all = kv_cols * tensor_size // (2 * head_dim)
    per_group = heads_all // kv_heads_all
    groups_dev = prefix_cache.shape[0]
    pre_local = prefix_cache.shape[1]
    suf_local = suffix_cache.shape[1]
    residual_all = lax.all_gather(residual_in, "tensor", axis=0, tiled=True)
    piece = rms_scale(residual_all.astype(jnp.float32), attn_gain).astype(jnp.bfloat16)
    projected = jnp.concatenate(
        [
            jnp.dot(piece, query_weight, preferred_element_type=jnp.float32),
            jnp.dot(piece, kv_weight, preferred_element_type=jnp.float32),
        ],
        axis=1,
    )
    query_raw = projected[:, :query_cols].reshape(requests, heads_here, head_dim)
    kv_raw = projected[:, query_cols:].reshape(requests, kv_cols // head_dim, head_dim)
    group_ids = dp_rank * groups_dev + jnp.arange(groups_dev)
    member = request_group[:, None] == group_ids[None, :]
    prefix_of = jnp.sum(jnp.where(member, prefix_len[None, :], 0), axis=1)
    positions = prefix_of + suffix_len
    queries = rotate(rms_scale(query_raw, query_gain), positions).astype(jnp.bfloat16)
    head_number = tensor_rank * (kv_cols // head_dim) + jnp.arange(kv_cols // head_dim)
    is_key = (head_number < kv_heads_all)[None, :, None]
    keyed = rotate(rms_scale(kv_raw, key_gain), positions)
    new_rows = jnp.where(is_key, keyed, kv_raw).astype(jnp.bfloat16).reshape(requests, kv_cols)
    joined = jnp.concatenate([queries.reshape(requests, query_cols), new_rows], axis=1)
    every_head = lax.all_gather(joined, "tensor", axis=1, tiled=True).reshape(
        requests, tensor_size, query_cols + kv_cols
    )
    all_queries = every_head[:, :, :query_cols].reshape(requests, kv_heads_all, per_group, head_dim)
    all_kv = every_head[:, :, query_cols:]
    own_keys = all_kv[:, :kv_heads_all]
    own_values = all_kv[:, kv_heads_all:].astype(jnp.float32)
    scale = 1.0 / math.sqrt(head_dim)
    split_at = kv_heads_all * head_dim
    pre_keys = prefix_cache[:, :, :split_at].reshape(groups_dev, pre_local, kv_heads_all, head_dim)
    pre_values = prefix_cache[:, :, split_at:].reshape(
        groups_dev, pre_local, kv_heads_all, head_dim
    )
    suf_keys = suffix_cache[:, :, :split_at].reshape(requests, suf_local, kv_heads_all, head_dim)
    suf_values = suffix_cache[:, :, split_at:].reshape(requests, suf_local, kv_heads_all, head_dim)
    pre_scores = (
        jnp.einsum("rgqd,npgd->rgqnp", all_queries, pre_keys, preferred_element_type=jnp.float32)
        * scale
    )
    suf_scores = (
        jnp.einsum("rgqd,rsgd->rgqs", all_queries, suf_keys, preferred_element_type=jnp.float32)
        * scale
    )
    own_scores = (
        jnp.einsum("rgqd,rgd->rgq", all_queries, own_keys, preferred_element_type=jnp.float32)
        * scale
    )
    pre_slots = tensor_rank * pre_local + jnp.arange(pre_local)
    pre_valid = (member[:, :, None] & (pre_slots[None, None, :] < prefix_len[None, :, None]))[
        :, None, None, :, :
    ]
    suf_slots = tensor_rank * suf_local + jnp.arange(suf_local)
    suf_valid = (suf_slots[None, :] < suffix_len[:, None])[:, None, None, :]
    own_valid = tensor_rank == 0
    top_pre = jnp.max(jnp.where(pre_valid, pre_scores, NEGATIVE), axis=(3, 4))
    top_suf = jnp.max(jnp.where(suf_valid, suf_scores, NEGATIVE), axis=3)
    top_own = jnp.where(own_valid, own_scores, NEGATIVE)
    top_local = (
        jnp.maximum(jnp.maximum(top_pre, top_suf), top_own).astype(jnp.bfloat16).astype(jnp.float32)
    )
    pre_weights = jnp.where(pre_valid, jnp.exp(pre_scores - top_local[..., None, None]), 0.0)
    suf_weights = jnp.where(suf_valid, jnp.exp(suf_scores - top_local[..., None]), 0.0)
    own_weights = jnp.where(own_valid, jnp.exp(own_scores - top_local), 0.0)
    total_local = jnp.sum(pre_weights, axis=(3, 4)) + jnp.sum(suf_weights, axis=3) + own_weights
    sums_local = jnp.einsum(
        "rgqnp,npgd->rgqd",
        pre_weights.astype(jnp.bfloat16),
        pre_values,
        preferred_element_type=jnp.float32,
    )
    sums_local = sums_local + jnp.einsum(
        "rgqs,rsgd->rgqd",
        suf_weights.astype(jnp.bfloat16),
        suf_values,
        preferred_element_type=jnp.float32,
    )
    own_low = own_weights.astype(jnp.bfloat16).astype(jnp.float32)
    sums_local = sums_local + own_low[..., None] * own_values[:, :, None, :]
    pair_rows = requests * heads_here // head_dim

    def by_owner(values):
        values = values.reshape(requests, tensor_size, heads_here, -1).transpose(1, 0, 2, 3)
        return values.reshape(tensor_size, -1, head_dim)

    total_high = total_local.astype(jnp.bfloat16)
    total_low = (total_local - total_high.astype(jnp.float32)).astype(jnp.bfloat16)
    packed = jnp.concatenate(
        [
            by_owner(sums_local.astype(jnp.bfloat16)),
            by_owner(top_local.astype(jnp.bfloat16)),
            by_owner(total_high),
            by_owner(total_low),
        ],
        axis=1,
    )
    parts = lax.all_to_all(packed, "tensor", 0, 0, tiled=True).astype(jnp.float32)
    spread = requests * heads_here
    part_sums = parts[:, :spread].reshape(tensor_size, requests, heads_here, head_dim)
    part_top = parts[:, spread : spread + pair_rows].reshape(tensor_size, requests, heads_here)
    part_total = (
        parts[:, spread + pair_rows : spread + 2 * pair_rows]
        + parts[:, spread + 2 * pair_rows :]
    ).reshape(tensor_size, requests, heads_here)
    top_all = jnp.max(part_top, axis=0)
    factor = jnp.exp(part_top - top_all[None])
    total_mine = jnp.sum(part_total * factor, axis=0)
    sums_mine = jnp.sum(part_sums * factor[..., None], axis=0)
    mixed = sums_mine / total_mine[..., None]
    attn_heads = mixed.reshape(requests, query_cols).astype(jnp.bfloat16)
    width_here = model_width // tensor_size
    tokens_here = residual_in.shape[0]
    attn_parts = lax.all_to_all(
        jnp.dot(attn_heads, out_weight, preferred_element_type=jnp.float32).astype(jnp.bfloat16),
        "tensor",
        split_axis=0,
        concat_axis=0,
        tiled=True,
    ).reshape(tensor_size, tokens_here, model_width)
    attn_out = jnp.sum(attn_parts.astype(jnp.float32), axis=0)
    middle = (residual_in.astype(jnp.float32) + attn_out).astype(jnp.bfloat16)
    moe_in = rms_scale(middle.astype(jnp.float32), moe_gain).astype(jnp.bfloat16)
    cols_in = lax.all_to_all(moe_in, "tensor", split_axis=1, concat_axis=0, tiled=True)
    local_experts = gate_weight.shape[0]
    experts_all = local_experts * owners
    topk = routes.shape[1]
    capacity = 2 * requests * topk // experts_all
    flat_routes = routes.reshape(-1)
    onehot = (flat_routes[:, None] == jnp.arange(experts_all)[None, :]).astype(jnp.int32)
    running = jnp.cumsum(onehot, axis=0)
    slot_of = jnp.sum(onehot * running, axis=1) - 1
    code_of = (flat_routes * capacity + slot_of).reshape(requests, topk)
    code_span = jnp.arange(experts_all * capacity)
    placing = jnp.any(code_of[None, :, :] == code_span[:, None, None], axis=2).astype(jnp.bfloat16)
    share = route_weights / jnp.sum(route_weights, axis=1, keepdims=True)
    placed = jnp.dot(placing, cols_in, preferred_element_type=jnp.float32)
    outgoing = placed.astype(jnp.bfloat16).reshape(owners, local_experts * capacity, width_here)
    arrived = lax.all_to_all(outgoing, "dp", split_axis=0, concat_axis=0, tiled=True)
    rows = lax.all_gather(arrived, "tensor", axis=2, tiled=True).reshape(
        owners, local_experts, capacity, model_width
    )
    gate_val = jnp.einsum("necd,edf->necf", rows, gate_weight, preferred_element_type=jnp.float32)
    lift_val = jnp.einsum("necd,edf->necf", rows, lift_weight, preferred_element_type=jnp.float32)
    hidden_units = (jax.nn.silu(gate_val) * lift_val).astype(jnp.bfloat16)
    hidden_all = lax.all_gather(hidden_units, "tensor", axis=0)
    ff_here = down_weight.shape[1]
    down_split = down_weight.reshape(local_experts, ff_here, tensor_size, width_here).transpose(
        2, 0, 1, 3
    )
    down_cols = lax.all_to_all(down_split, "tensor", 0, 0, tiled=True)
    summed_out = jnp.einsum(
        "tnecf,tefd->necd", hidden_all, down_cols, preferred_element_type=jnp.float32
    ).astype(jnp.bfloat16)
    returned = lax.all_to_all(
        summed_out.reshape(owners, local_experts * capacity, width_here),
        "dp",
        split_axis=0,
        concat_axis=0,
        tiled=True,
    ).astype(jnp.float32)
    returned = returned.reshape(experts_all * capacity, width_here)
    picked_rows = returned[code_of]
    moe_cols = jnp.sum(share[:, :, None] * picked_rows, axis=1).astype(jnp.bfloat16)
    moe_out = lax.all_to_all(moe_cols, "tensor", split_axis=0, concat_axis=1, tiled=True)
    layer_out = (middle.astype(jnp.float32) + moe_out.astype(jnp.float32)).astype(jnp.bfloat16)
    return (layer_out, new_rows)


def solution(mesh):
    in_specs = (
        P(("dp", "tensor"), None),
        P(),
        P(None, "tensor"),
        P(None, "tensor"),
        P(),
        P(),
        P("tensor", None),
        P(),
        P("dp", None, "tensor"),
        P("dp", None, "tensor"),
        P("dp", "tensor", None),
        P("dp", None),
        P("dp", None),
        P("dp", "tensor", None),
        P("dp", "tensor", None),
        P("dp"),
        P("dp"),
        P("dp"),
    )
    out_specs = (P(("dp", "tensor"), None), P("dp", "tensor"))
    return jax.shard_map(body, mesh=mesh, in_specs=in_specs, out_specs=out_specs, check_vma=False)
```

```python
import math

import jax
import jax.numpy as jnp
from jax import lax
from jax.sharding import PartitionSpec as P

EPSILON = 1e-06
THETA = 1000000.0
NEGATIVE = -1e30


def rms_scale(values, gain):
    mean_square = jnp.mean(values * values, axis=-1, keepdims=True)
    return values * lax.rsqrt(mean_square + EPSILON) * gain


def rotate(values, positions):
    half = values.shape[-1] // 2
    freqs = THETA ** (-jnp.arange(half).astype(jnp.float32) * 2.0 / values.shape[-1])
    angles = positions.astype(jnp.float32)[:, None] * freqs[None, :]
    angles = jnp.concatenate([angles, angles], axis=-1)
    cosine = jnp.cos(angles)[:, None, :]
    sine = jnp.sin(angles)[:, None, :]
    turned = jnp.concatenate([-values[..., half:], values[..., :half]], axis=-1)
    return values * cosine + turned * sine


def body(
    residual_in,
    attn_gain,
    query_weight,
    kv_weight,
    query_gain,
    key_gain,
    out_weight,
    moe_gain,
    gate_weight,
    lift_weight,
    down_weight,
    routes,
    route_weights,
    prefix_cache,
    suffix_cache,
    prefix_len,
    suffix_len,
    request_group,
):
    tensor_size = lax.axis_size("tensor")
    tensor_rank = lax.axis_index("tensor")
    dp_rank = lax.axis_index("dp")
    owners = lax.axis_size("dp")
    head_dim = query_gain.shape[0]
    requests = routes.shape[0]
    model_width = residual_in.shape[1]
    query_cols = query_weight.shape[1]
    kv_cols = kv_weight.shape[1]
    heads_here = query_cols // head_dim
    heads_all = heads_here * tensor_size
    kv_heads_all = kv_cols * tensor_size // (2 * head_dim)
    per_group = heads_all // kv_heads_all
    groups_dev = prefix_cache.shape[0]
    pre_local = prefix_cache.shape[1]
    suf_local = suffix_cache.shape[1]
    residual_all = lax.all_gather(residual_in, "tensor", axis=0, tiled=True)
    piece = rms_scale(residual_all.astype(jnp.float32), attn_gain).astype(jnp.bfloat16)
    projected = jnp.concatenate(
        [
            jnp.dot(piece, query_weight, preferred_element_type=jnp.float32),
            jnp.dot(piece, kv_weight, preferred_element_type=jnp.float32),
        ],
        axis=1,
    )
    query_raw = projected[:, :query_cols].reshape(requests, heads_here, head_dim)
    kv_raw = projected[:, query_cols:].reshape(requests, kv_cols // head_dim, head_dim)
    group_ids = dp_rank * groups_dev + jnp.arange(groups_dev)
    member = request_group[:, None] == group_ids[None, :]
    prefix_of = jnp.sum(jnp.where(member, prefix_len[None, :], 0), axis=1)
    positions = prefix_of + suffix_len
    queries = rotate(rms_scale(query_raw, query_gain), positions).astype(jnp.bfloat16)
    head_number = tensor_rank * (kv_cols // head_dim) + jnp.arange(kv_cols // head_dim)
    is_key = (head_number < kv_heads_all)[None, :, None]
    keyed = rotate(rms_scale(kv_raw, key_gain), positions)
    new_rows = jnp.where(is_key, keyed, kv_raw).astype(jnp.bfloat16).reshape(requests, kv_cols)
    joined = jnp.concatenate([queries.reshape(requests, query_cols), new_rows], axis=1)
    every_head = lax.all_gather(joined, "tensor", axis=1, tiled=True).reshape(
        requests, tensor_size, query_cols + kv_cols
    )
    all_queries = every_head[:, :, :query_cols].reshape(requests, kv_heads_all, per_group, head_dim)
    all_kv = every_head[:, :, query_cols:]
    own_keys = all_kv[:, :kv_heads_all]
    own_values = all_kv[:, kv_heads_all:].astype(jnp.float32)
    scale = 1.0 / math.sqrt(head_dim)
    split_at = kv_heads_all * head_dim
    pre_keys = prefix_cache[:, :, :split_at].reshape(groups_dev, pre_local, kv_heads_all, head_dim)
    pre_values = prefix_cache[:, :, split_at:].reshape(
        groups_dev, pre_local, kv_heads_all, head_dim
    )
    suf_keys = suffix_cache[:, :, :split_at].reshape(requests, suf_local, kv_heads_all, head_dim)
    suf_values = suffix_cache[:, :, split_at:].reshape(requests, suf_local, kv_heads_all, head_dim)
    pre_scores = (
        jnp.einsum("rgqd,npgd->rgqnp", all_queries, pre_keys, preferred_element_type=jnp.float32)
        * scale
    )
    suf_scores = (
        jnp.einsum("rgqd,rsgd->rgqs", all_queries, suf_keys, preferred_element_type=jnp.float32)
        * scale
    )
    own_scores = (
        jnp.einsum("rgqd,rgd->rgq", all_queries, own_keys, preferred_element_type=jnp.float32)
        * scale
    )
    pre_slots = tensor_rank * pre_local + jnp.arange(pre_local)
    pre_valid = (member[:, :, None] & (pre_slots[None, None, :] < prefix_len[None, :, None]))[
        :, None, None, :, :
    ]
    suf_slots = tensor_rank * suf_local + jnp.arange(suf_local)
    suf_valid = (suf_slots[None, :] < suffix_len[:, None])[:, None, None, :]
    own_valid = tensor_rank == 0
    top_pre = jnp.max(jnp.where(pre_valid, pre_scores, NEGATIVE), axis=(3, 4))
    top_suf = jnp.max(jnp.where(suf_valid, suf_scores, NEGATIVE), axis=3)
    top_own = jnp.where(own_valid, own_scores, NEGATIVE)
    top_local = (
        jnp.maximum(jnp.maximum(top_pre, top_suf), top_own).astype(jnp.bfloat16).astype(jnp.float32)
    )
    pre_weights = jnp.where(pre_valid, jnp.exp(pre_scores - top_local[..., None, None]), 0.0)
    suf_weights = jnp.where(suf_valid, jnp.exp(suf_scores - top_local[..., None]), 0.0)
    own_weights = jnp.where(own_valid, jnp.exp(own_scores - top_local), 0.0)
    total_local = jnp.sum(pre_weights, axis=(3, 4)) + jnp.sum(suf_weights, axis=3) + own_weights
    sums_local = jnp.einsum(
        "rgqnp,npgd->rgqd",
        pre_weights.astype(jnp.bfloat16),
        pre_values,
        preferred_element_type=jnp.float32,
    )
    sums_local = sums_local + jnp.einsum(
        "rgqs,rsgd->rgqd",
        suf_weights.astype(jnp.bfloat16),
        suf_values,
        preferred_element_type=jnp.float32,
    )
    own_low = own_weights.astype(jnp.bfloat16).astype(jnp.float32)
    sums_local = sums_local + own_low[..., None] * own_values[:, :, None, :]
    pair_rows = requests * heads_here // head_dim

    def by_owner(values):
        values = values.reshape(requests, tensor_size, heads_here, -1).transpose(1, 0, 2, 3)
        return values.reshape(tensor_size, -1, head_dim)

    total_high = total_local.astype(jnp.bfloat16)
    total_low = (total_local - total_high.astype(jnp.float32)).astype(jnp.bfloat16)
    packed = jnp.concatenate(
        [
            by_owner(sums_local.astype(jnp.bfloat16)),
            by_owner(top_local.astype(jnp.bfloat16)),
            by_owner(total_high),
            by_owner(total_low),
        ],
        axis=1,
    )
    parts = lax.all_to_all(packed, "tensor", 0, 0, tiled=True).astype(jnp.float32)
    spread = requests * heads_here
    part_sums = parts[:, :spread].reshape(tensor_size, requests, heads_here, head_dim)
    part_top = parts[:, spread : spread + pair_rows].reshape(tensor_size, requests, heads_here)
    part_total = (
        parts[:, spread + pair_rows : spread + 2 * pair_rows]
        + parts[:, spread + 2 * pair_rows :]
    ).reshape(tensor_size, requests, heads_here)
    top_all = jnp.max(part_top, axis=0)
    factor = jnp.exp(part_top - top_all[None])
    total_mine = jnp.sum(part_total * factor, axis=0)
    sums_mine = jnp.sum(part_sums * factor[..., None], axis=0)
    mixed = sums_mine / total_mine[..., None]
    attn_heads = mixed.reshape(requests, query_cols).astype(jnp.bfloat16)
    width_here = model_width // tensor_size
    tokens_here = residual_in.shape[0]
    attn_parts = lax.all_to_all(
        jnp.dot(attn_heads, out_weight, preferred_element_type=jnp.float32).astype(jnp.bfloat16),
        "tensor",
        split_axis=0,
        concat_axis=0,
        tiled=True,
    ).reshape(tensor_size, tokens_here, model_width)
    attn_out = jnp.sum(attn_parts.astype(jnp.float32), axis=0)
    middle = (residual_in.astype(jnp.float32) + attn_out).astype(jnp.bfloat16)
    moe_in = rms_scale(middle.astype(jnp.float32), moe_gain).astype(jnp.bfloat16)
    cols_in = lax.all_to_all(moe_in, "tensor", split_axis=1, concat_axis=0, tiled=True)
    local_experts = gate_weight.shape[0]
    experts_all = local_experts * owners
    topk = routes.shape[1]
    capacity = 2 * requests * topk // experts_all
    flat_routes = routes.reshape(-1)
    onehot = (flat_routes[:, None] == jnp.arange(experts_all)[None, :]).astype(jnp.int32)
    running = jnp.cumsum(onehot, axis=0)
    slot_of = jnp.sum(onehot * running, axis=1) - 1
    code_of = (flat_routes * capacity + slot_of).reshape(requests, topk)
    code_span = jnp.arange(experts_all * capacity)
    placing = jnp.any(code_of[None, :, :] == code_span[:, None, None], axis=2).astype(jnp.bfloat16)
    share = route_weights / jnp.sum(route_weights, axis=1, keepdims=True)
    placed = jnp.dot(placing, cols_in, preferred_element_type=jnp.float32)
    outgoing = placed.astype(jnp.bfloat16).reshape(owners, local_experts * capacity, width_here)
    arrived = lax.all_to_all(outgoing, "dp", split_axis=0, concat_axis=0, tiled=True)
    rows = lax.all_gather(arrived, "tensor", axis=2, tiled=True).reshape(
        owners, local_experts, capacity, model_width
    )
    ff_here = down_weight.shape[1]
    down_split = down_weight.reshape(local_experts, ff_here, tensor_size, width_here).transpose(
        2, 0, 1, 3
    )
    down_cols = lax.all_to_all(down_split, "tensor", 0, 0, tiled=True)
    rows, down_cols = lax.optimization_barrier((rows, down_cols))
    gate_val = jnp.einsum("necd,edf->necf", rows, gate_weight, preferred_element_type=jnp.float32)
    lift_val = jnp.einsum("necd,edf->necf", rows, lift_weight, preferred_element_type=jnp.float32)
    hidden_units = (jax.nn.silu(gate_val) * lift_val).astype(jnp.bfloat16)
    hidden_all = lax.all_gather(hidden_units, "tensor", axis=0)
    summed_out = jnp.einsum(
        "tnecf,tefd->necd", hidden_all, down_cols, preferred_element_type=jnp.float32
    ).astype(jnp.bfloat16)
    returned = lax.all_to_all(
        summed_out.reshape(owners, local_experts * capacity, width_here),
        "dp",
        split_axis=0,
        concat_axis=0,
        tiled=True,
    ).astype(jnp.float32)
    returned = returned.reshape(experts_all * capacity, width_here)
    picked_rows = returned[code_of]
    moe_cols = jnp.sum(share[:, :, None] * picked_rows, axis=1).astype(jnp.bfloat16)
    moe_out = lax.all_to_all(moe_cols, "tensor", split_axis=0, concat_axis=1, tiled=True)
    layer_out = (middle.astype(jnp.float32) + moe_out.astype(jnp.float32)).astype(jnp.bfloat16)
    return (layer_out, new_rows)


def solution(mesh):
    in_specs = (
        P(("dp", "tensor"), None),
        P(),
        P(None, "tensor"),
        P(None, "tensor"),
        P(),
        P(),
        P("tensor", None),
        P(),
        P("dp", None, "tensor"),
        P("dp", None, "tensor"),
        P("dp", "tensor", None),
        P("dp", None),
        P("dp", None),
        P("dp", "tensor", None),
        P("dp", "tensor", None),
        P("dp"),
        P("dp"),
        P("dp"),
    )
    out_specs = (P(("dp", "tensor"), None), P("dp", "tensor"))
    return jax.shard_map(body, mesh=mesh, in_specs=in_specs, out_specs=out_specs, check_vma=False)
```

```python
import math

import jax
import jax.numpy as jnp
from jax import lax
from jax.sharding import PartitionSpec as P

EPSILON = 1e-06
THETA = 1000000.0
NEGATIVE = -1e30


def rms_scale(values, gain):
    mean_square = jnp.mean(values * values, axis=-1, keepdims=True)
    return values * lax.rsqrt(mean_square + EPSILON) * gain


def rotate(values, positions):
    half = values.shape[-1] // 2
    freqs = THETA ** (-jnp.arange(half).astype(jnp.float32) * 2.0 / values.shape[-1])
    angles = positions.astype(jnp.float32)[:, None] * freqs[None, :]
    angles = jnp.concatenate([angles, angles], axis=-1)
    cosine = jnp.cos(angles)[:, None, :]
    sine = jnp.sin(angles)[:, None, :]
    turned = jnp.concatenate([-values[..., half:], values[..., :half]], axis=-1)
    return values * cosine + turned * sine


def body(
    residual_in,
    attn_gain,
    query_weight,
    kv_weight,
    query_gain,
    key_gain,
    out_weight,
    moe_gain,
    gate_weight,
    lift_weight,
    down_weight,
    routes,
    route_weights,
    prefix_cache,
    suffix_cache,
    prefix_len,
    suffix_len,
    request_group,
):
    tensor_size = lax.axis_size("tensor")
    tensor_rank = lax.axis_index("tensor")
    dp_rank = lax.axis_index("dp")
    owners = lax.axis_size("dp")
    head_dim = query_gain.shape[0]
    requests = routes.shape[0]
    model_width = residual_in.shape[1]
    query_cols = query_weight.shape[1]
    kv_cols = kv_weight.shape[1]
    heads_here = query_cols // head_dim
    heads_all = heads_here * tensor_size
    kv_heads_all = kv_cols * tensor_size // (2 * head_dim)
    per_group = heads_all // kv_heads_all
    groups_dev = prefix_cache.shape[0]
    pre_local = prefix_cache.shape[1]
    suf_local = suffix_cache.shape[1]
    residual_all = lax.all_to_all(
        jnp.broadcast_to(residual_in[None], (tensor_size,) + residual_in.shape),
        "tensor",
        0,
        0,
        tiled=True,
    ).reshape(-1, residual_in.shape[1])
    piece = rms_scale(residual_all.astype(jnp.float32), attn_gain).astype(jnp.bfloat16)
    projected = jnp.concatenate(
        [
            jnp.dot(piece, query_weight, preferred_element_type=jnp.float32),
            jnp.dot(piece, kv_weight, preferred_element_type=jnp.float32),
        ],
        axis=1,
    )
    query_raw = projected[:, :query_cols].reshape(requests, heads_here, head_dim)
    kv_raw = projected[:, query_cols:].reshape(requests, kv_cols // head_dim, head_dim)
    group_ids = dp_rank * groups_dev + jnp.arange(groups_dev)
    member = request_group[:, None] == group_ids[None, :]
    prefix_of = jnp.sum(jnp.where(member, prefix_len[None, :], 0), axis=1)
    positions = prefix_of + suffix_len
    queries = rotate(rms_scale(query_raw, query_gain), positions).astype(jnp.bfloat16)
    head_number = tensor_rank * (kv_cols // head_dim) + jnp.arange(kv_cols // head_dim)
    is_key = (head_number < kv_heads_all)[None, :, None]
    keyed = rotate(rms_scale(kv_raw, key_gain), positions)
    new_rows = jnp.where(is_key, keyed, kv_raw).astype(jnp.bfloat16).reshape(requests, kv_cols)
    joined = jnp.concatenate([queries.reshape(requests, query_cols), new_rows], axis=1)
    every_head = lax.all_to_all(
        jnp.broadcast_to(joined[None], (tensor_size,) + joined.shape), "tensor", 0, 0, tiled=True
    ).transpose(1, 0, 2)
    all_queries = every_head[:, :, :query_cols].reshape(requests, kv_heads_all, per_group, head_dim)
    all_kv = every_head[:, :, query_cols:]
    own_keys = all_kv[:, :kv_heads_all]
    own_values = all_kv[:, kv_heads_all:].astype(jnp.float32)
    scale = 1.0 / math.sqrt(head_dim)
    split_at = kv_heads_all * head_dim
    pre_keys = prefix_cache[:, :, :split_at].reshape(groups_dev, pre_local, kv_heads_all, head_dim)
    pre_values = prefix_cache[:, :, split_at:].reshape(
        groups_dev, pre_local, kv_heads_all, head_dim
    )
    suf_keys = suffix_cache[:, :, :split_at].reshape(requests, suf_local, kv_heads_all, head_dim)
    suf_values = suffix_cache[:, :, split_at:].reshape(requests, suf_local, kv_heads_all, head_dim)
    pre_scores = (
        jnp.einsum("rgqd,npgd->rgqnp", all_queries, pre_keys, preferred_element_type=jnp.float32)
        * scale
    )
    suf_scores = (
        jnp.einsum("rgqd,rsgd->rgqs", all_queries, suf_keys, preferred_element_type=jnp.float32)
        * scale
    )
    own_scores = (
        jnp.einsum("rgqd,rgd->rgq", all_queries, own_keys, preferred_element_type=jnp.float32)
        * scale
    )
    pre_slots = tensor_rank * pre_local + jnp.arange(pre_local)
    pre_valid = (member[:, :, None] & (pre_slots[None, None, :] < prefix_len[None, :, None]))[
        :, None, None, :, :
    ]
    suf_slots = tensor_rank * suf_local + jnp.arange(suf_local)
    suf_valid = (suf_slots[None, :] < suffix_len[:, None])[:, None, None, :]
    own_valid = tensor_rank == 0
    top_pre = jnp.max(jnp.where(pre_valid, pre_scores, NEGATIVE), axis=(3, 4))
    top_suf = jnp.max(jnp.where(suf_valid, suf_scores, NEGATIVE), axis=3)
    top_own = jnp.where(own_valid, own_scores, NEGATIVE)
    top_local = (
        jnp.maximum(jnp.maximum(top_pre, top_suf), top_own).astype(jnp.bfloat16).astype(jnp.float32)
    )
    pre_weights = jnp.where(pre_valid, jnp.exp(pre_scores - top_local[..., None, None]), 0.0)
    suf_weights = jnp.where(suf_valid, jnp.exp(suf_scores - top_local[..., None]), 0.0)
    own_weights = jnp.where(own_valid, jnp.exp(own_scores - top_local), 0.0)
    total_local = jnp.sum(pre_weights, axis=(3, 4)) + jnp.sum(suf_weights, axis=3) + own_weights
    sums_local = jnp.einsum(
        "rgqnp,npgd->rgqd",
        pre_weights.astype(jnp.bfloat16),
        pre_values,
        preferred_element_type=jnp.float32,
    )
    sums_local = sums_local + jnp.einsum(
        "rgqs,rsgd->rgqd",
        suf_weights.astype(jnp.bfloat16),
        suf_values,
        preferred_element_type=jnp.float32,
    )
    own_low = own_weights.astype(jnp.bfloat16).astype(jnp.float32)
    sums_local = sums_local + own_low[..., None] * own_values[:, :, None, :]
    pair_rows = requests * heads_here // head_dim

    def by_owner(values):
        values = values.reshape(requests, tensor_size, heads_here, -1).transpose(1, 0, 2, 3)
        return values.reshape(tensor_size, -1, head_dim)

    total_high = total_local.astype(jnp.bfloat16)
    total_low = (total_local - total_high.astype(jnp.float32)).astype(jnp.bfloat16)
    packed = jnp.concatenate(
        [
            by_owner(sums_local.astype(jnp.bfloat16)),
            by_owner(top_local.astype(jnp.bfloat16)),
            by_owner(total_high),
            by_owner(total_low),
        ],
        axis=1,
    )
    parts = lax.all_to_all(packed, "tensor", 0, 0, tiled=True).astype(jnp.float32)
    spread = requests * heads_here
    part_sums = parts[:, :spread].reshape(tensor_size, requests, heads_here, head_dim)
    part_top = parts[:, spread : spread + pair_rows].reshape(tensor_size, requests, heads_here)
    part_total = (
        parts[:, spread + pair_rows : spread + 2 * pair_rows]
        + parts[:, spread + 2 * pair_rows :]
    ).reshape(tensor_size, requests, heads_here)
    top_all = jnp.max(part_top, axis=0)
    factor = jnp.exp(part_top - top_all[None])
    total_mine = jnp.sum(part_total * factor, axis=0)
    sums_mine = jnp.sum(part_sums * factor[..., None], axis=0)
    mixed = sums_mine / total_mine[..., None]
    attn_heads = mixed.reshape(requests, query_cols).astype(jnp.bfloat16)
    width_here = model_width // tensor_size
    tokens_here = residual_in.shape[0]
    attn_parts = lax.all_to_all(
        jnp.dot(attn_heads, out_weight, preferred_element_type=jnp.float32).astype(jnp.bfloat16),
        "tensor",
        split_axis=0,
        concat_axis=0,
        tiled=True,
    ).reshape(tensor_size, tokens_here, model_width)
    attn_out = jnp.sum(attn_parts.astype(jnp.float32), axis=0)
    middle = (residual_in.astype(jnp.float32) + attn_out).astype(jnp.bfloat16)
    moe_in = rms_scale(middle.astype(jnp.float32), moe_gain).astype(jnp.bfloat16)
    cols_in = lax.all_to_all(moe_in, "tensor", split_axis=1, concat_axis=0, tiled=True)
    local_experts = gate_weight.shape[0]
    experts_all = local_experts * owners
    topk = routes.shape[1]
    capacity = 2 * requests * topk // experts_all
    flat_routes = routes.reshape(-1)
    onehot = (flat_routes[:, None] == jnp.arange(experts_all)[None, :]).astype(jnp.int32)
    running = jnp.cumsum(onehot, axis=0)
    slot_of = jnp.sum(onehot * running, axis=1) - 1
    code_of = (flat_routes * capacity + slot_of).reshape(requests, topk)
    code_span = jnp.arange(experts_all * capacity)
    placing = jnp.any(code_of[None, :, :] == code_span[:, None, None], axis=2).astype(jnp.bfloat16)
    share = route_weights / jnp.sum(route_weights, axis=1, keepdims=True)
    placed = jnp.dot(placing, cols_in, preferred_element_type=jnp.float32)
    outgoing = placed.astype(jnp.bfloat16).reshape(owners, local_experts * capacity, width_here)
    arrived = lax.all_to_all(outgoing, "dp", split_axis=0, concat_axis=0, tiled=True)
    rows = lax.all_gather(arrived, "tensor", axis=2, tiled=True).reshape(
        owners, local_experts, capacity, model_width
    )
    gate_val = jnp.einsum("necd,edf->necf", rows, gate_weight, preferred_element_type=jnp.float32)
    lift_val = jnp.einsum("necd,edf->necf", rows, lift_weight, preferred_element_type=jnp.float32)
    hidden_units = (jax.nn.silu(gate_val) * lift_val).astype(jnp.bfloat16)
    hidden_all = lax.all_gather(hidden_units, "tensor", axis=0)
    ff_here = down_weight.shape[1]
    down_split = down_weight.reshape(local_experts, ff_here, tensor_size, width_here).transpose(
        2, 0, 1, 3
    )
    down_cols = lax.all_to_all(down_split, "tensor", 0, 0, tiled=True)
    summed_out = jnp.einsum(
        "tnecf,tefd->necd", hidden_all, down_cols, preferred_element_type=jnp.float32
    ).astype(jnp.bfloat16)
    returned = lax.all_to_all(
        summed_out.reshape(owners, local_experts * capacity, width_here),
        "dp",
        split_axis=0,
        concat_axis=0,
        tiled=True,
    ).astype(jnp.float32)
    returned = returned.reshape(experts_all * capacity, width_here)
    picked_rows = returned[code_of]
    moe_cols = jnp.sum(share[:, :, None] * picked_rows, axis=1).astype(jnp.bfloat16)
    moe_out = lax.all_to_all(moe_cols, "tensor", split_axis=0, concat_axis=1, tiled=True)
    layer_out = (middle.astype(jnp.float32) + moe_out.astype(jnp.float32)).astype(jnp.bfloat16)
    return (layer_out, new_rows)


def solution(mesh):
    in_specs = (
        P(("dp", "tensor"), None),
        P(),
        P(None, "tensor"),
        P(None, "tensor"),
        P(),
        P(),
        P("tensor", None),
        P(),
        P("dp", None, "tensor"),
        P("dp", None, "tensor"),
        P("dp", "tensor", None),
        P("dp", None),
        P("dp", None),
        P("dp", "tensor", None),
        P("dp", "tensor", None),
        P("dp"),
        P("dp"),
        P("dp"),
    )
    out_specs = (P(("dp", "tensor"), None), P("dp", "tensor"))
    return jax.shard_map(body, mesh=mesh, in_specs=in_specs, out_specs=out_specs, check_vma=False)
```

```python
import math

import jax
import jax.numpy as jnp
from jax import lax
from jax.sharding import PartitionSpec as P

EPSILON = 1e-06
THETA = 1000000.0
NEGATIVE = -1e30


def rms_scale(values, gain):
    mean_square = jnp.mean(values * values, axis=-1, keepdims=True)
    return values * lax.rsqrt(mean_square + EPSILON) * gain


def rotate(values, positions):
    half = values.shape[-1] // 2
    freqs = THETA ** (-jnp.arange(half).astype(jnp.float32) * 2.0 / values.shape[-1])
    angles = positions.astype(jnp.float32)[:, None] * freqs[None, :]
    angles = jnp.concatenate([angles, angles], axis=-1)
    cosine = jnp.cos(angles)[:, None, :]
    sine = jnp.sin(angles)[:, None, :]
    turned = jnp.concatenate([-values[..., half:], values[..., :half]], axis=-1)
    return values * cosine + turned * sine


def body(
    residual_in,
    attn_gain,
    query_weight,
    kv_weight,
    query_gain,
    key_gain,
    out_weight,
    moe_gain,
    gate_weight,
    lift_weight,
    down_weight,
    routes,
    route_weights,
    prefix_cache,
    suffix_cache,
    prefix_len,
    suffix_len,
    request_group,
):
    tensor_size = lax.axis_size("tensor")
    tensor_rank = lax.axis_index("tensor")
    dp_rank = lax.axis_index("dp")
    owners = lax.axis_size("dp")
    head_dim = query_gain.shape[0]
    requests = routes.shape[0]
    model_width = residual_in.shape[1]
    query_cols = query_weight.shape[1]
    kv_cols = kv_weight.shape[1]
    heads_here = query_cols // head_dim
    heads_all = heads_here * tensor_size
    kv_heads_all = kv_cols * tensor_size // (2 * head_dim)
    per_group = heads_all // kv_heads_all
    groups_dev = prefix_cache.shape[0]
    pre_local = prefix_cache.shape[1]
    suf_local = suffix_cache.shape[1]
    residual_all = lax.all_to_all(
        jnp.broadcast_to(residual_in[None], (tensor_size,) + residual_in.shape),
        "tensor",
        0,
        0,
        tiled=True,
    ).reshape(-1, residual_in.shape[1])
    piece = rms_scale(residual_all.astype(jnp.float32), attn_gain).astype(jnp.bfloat16)
    projected = jnp.concatenate(
        [
            jnp.dot(piece, query_weight, preferred_element_type=jnp.float32),
            jnp.dot(piece, kv_weight, preferred_element_type=jnp.float32),
        ],
        axis=1,
    )
    query_raw = projected[:, :query_cols].reshape(requests, heads_here, head_dim)
    kv_raw = projected[:, query_cols:].reshape(requests, kv_cols // head_dim, head_dim)
    group_ids = dp_rank * groups_dev + jnp.arange(groups_dev)
    member = request_group[:, None] == group_ids[None, :]
    prefix_of = jnp.sum(jnp.where(member, prefix_len[None, :], 0), axis=1)
    positions = prefix_of + suffix_len
    queries = rotate(rms_scale(query_raw, query_gain), positions).astype(jnp.bfloat16)
    head_number = tensor_rank * (kv_cols // head_dim) + jnp.arange(kv_cols // head_dim)
    is_key = (head_number < kv_heads_all)[None, :, None]
    keyed = rotate(rms_scale(kv_raw, key_gain), positions)
    new_rows = jnp.where(is_key, keyed, kv_raw).astype(jnp.bfloat16).reshape(requests, kv_cols)
    joined = jnp.concatenate([queries.reshape(requests, query_cols), new_rows], axis=1)
    every_head = lax.all_to_all(
        jnp.broadcast_to(joined[None], (tensor_size,) + joined.shape), "tensor", 0, 0, tiled=True
    ).transpose(1, 0, 2)
    all_queries = every_head[:, :, :query_cols].reshape(requests, kv_heads_all, per_group, head_dim)
    all_kv = every_head[:, :, query_cols:]
    own_keys = all_kv[:, :kv_heads_all]
    own_values = all_kv[:, kv_heads_all:].astype(jnp.float32)
    scale = 1.0 / math.sqrt(head_dim)
    split_at = kv_heads_all * head_dim
    pre_keys = prefix_cache[:, :, :split_at].reshape(groups_dev, pre_local, kv_heads_all, head_dim)
    pre_values = prefix_cache[:, :, split_at:].reshape(
        groups_dev, pre_local, kv_heads_all, head_dim
    )
    suf_keys = suffix_cache[:, :, :split_at].reshape(requests, suf_local, kv_heads_all, head_dim)
    suf_values = suffix_cache[:, :, split_at:].reshape(requests, suf_local, kv_heads_all, head_dim)
    pre_scores = (
        jnp.einsum("rgqd,npgd->rgqnp", all_queries, pre_keys, preferred_element_type=jnp.float32)
        * scale
    )
    suf_scores = (
        jnp.einsum("rgqd,rsgd->rgqs", all_queries, suf_keys, preferred_element_type=jnp.float32)
        * scale
    )
    own_scores = (
        jnp.einsum("rgqd,rgd->rgq", all_queries, own_keys, preferred_element_type=jnp.float32)
        * scale
    )
    pre_slots = tensor_rank * pre_local + jnp.arange(pre_local)
    pre_valid = (member[:, :, None] & (pre_slots[None, None, :] < prefix_len[None, :, None]))[
        :, None, None, :, :
    ]
    suf_slots = tensor_rank * suf_local + jnp.arange(suf_local)
    suf_valid = (suf_slots[None, :] < suffix_len[:, None])[:, None, None, :]
    own_valid = tensor_rank == 0
    top_pre = jnp.max(jnp.where(pre_valid, pre_scores, NEGATIVE), axis=(3, 4))
    top_suf = jnp.max(jnp.where(suf_valid, suf_scores, NEGATIVE), axis=3)
    top_own = jnp.where(own_valid, own_scores, NEGATIVE)
    top_local = (
        jnp.maximum(jnp.maximum(top_pre, top_suf), top_own).astype(jnp.bfloat16).astype(jnp.float32)
    )
    pre_weights = jnp.where(pre_valid, jnp.exp(pre_scores - top_local[..., None, None]), 0.0)
    suf_weights = jnp.where(suf_valid, jnp.exp(suf_scores - top_local[..., None]), 0.0)
    own_weights = jnp.where(own_valid, jnp.exp(own_scores - top_local), 0.0)
    total_local = jnp.sum(pre_weights, axis=(3, 4)) + jnp.sum(suf_weights, axis=3) + own_weights
    sums_local = jnp.einsum(
        "rgqnp,npgd->rgqd",
        pre_weights.astype(jnp.bfloat16),
        pre_values,
        preferred_element_type=jnp.float32,
    )
    sums_local = sums_local + jnp.einsum(
        "rgqs,rsgd->rgqd",
        suf_weights.astype(jnp.bfloat16),
        suf_values,
        preferred_element_type=jnp.float32,
    )
    own_low = own_weights.astype(jnp.bfloat16).astype(jnp.float32)
    sums_local = sums_local + own_low[..., None] * own_values[:, :, None, :]
    pair_rows = requests * heads_here // head_dim

    def by_owner(values):
        values = values.reshape(requests, tensor_size, heads_here, -1).transpose(1, 0, 2, 3)
        return values.reshape(tensor_size, -1, head_dim)

    total_high = total_local.astype(jnp.bfloat16)
    total_low = (total_local - total_high.astype(jnp.float32)).astype(jnp.bfloat16)
    packed = jnp.concatenate(
        [
            by_owner(sums_local.astype(jnp.bfloat16)),
            by_owner(top_local.astype(jnp.bfloat16)),
            by_owner(total_high),
            by_owner(total_low),
        ],
        axis=1,
    )
    parts = lax.all_to_all(packed, "tensor", 0, 0, tiled=True).astype(jnp.float32)
    spread = requests * heads_here
    part_sums = parts[:, :spread].reshape(tensor_size, requests, heads_here, head_dim)
    part_top = parts[:, spread : spread + pair_rows].reshape(tensor_size, requests, heads_here)
    part_total = (
        parts[:, spread + pair_rows : spread + 2 * pair_rows]
        + parts[:, spread + 2 * pair_rows :]
    ).reshape(tensor_size, requests, heads_here)
    top_all = jnp.max(part_top, axis=0)
    factor = jnp.exp(part_top - top_all[None])
    total_mine = jnp.sum(part_total * factor, axis=0)
    sums_mine = jnp.sum(part_sums * factor[..., None], axis=0)
    mixed = sums_mine / total_mine[..., None]
    attn_heads = mixed.reshape(requests, query_cols).astype(jnp.bfloat16)
    width_here = model_width // tensor_size
    tokens_here = residual_in.shape[0]
    attn_parts = lax.all_to_all(
        jnp.dot(attn_heads, out_weight, preferred_element_type=jnp.float32).astype(jnp.bfloat16),
        "tensor",
        split_axis=0,
        concat_axis=0,
        tiled=True,
    ).reshape(tensor_size, tokens_here, model_width)
    attn_out = jnp.sum(attn_parts.astype(jnp.float32), axis=0)
    middle = (residual_in.astype(jnp.float32) + attn_out).astype(jnp.bfloat16)
    moe_in = rms_scale(middle.astype(jnp.float32), moe_gain).astype(jnp.bfloat16)
    cols_in = lax.all_to_all(moe_in, "tensor", split_axis=1, concat_axis=0, tiled=True)
    local_experts = gate_weight.shape[0]
    experts_all = local_experts * owners
    topk = routes.shape[1]
    capacity = 2 * requests * topk // experts_all
    flat_routes = routes.reshape(-1)
    onehot = (flat_routes[:, None] == jnp.arange(experts_all)[None, :]).astype(jnp.int32)
    running = jnp.cumsum(onehot, axis=0)
    slot_of = jnp.sum(onehot * running, axis=1) - 1
    code_of = (flat_routes * capacity + slot_of).reshape(requests, topk)
    code_span = jnp.arange(experts_all * capacity)
    placing = jnp.any(code_of[None, :, :] == code_span[:, None, None], axis=2).astype(jnp.bfloat16)
    share = route_weights / jnp.sum(route_weights, axis=1, keepdims=True)
    placed = jnp.dot(placing, cols_in, preferred_element_type=jnp.float32)
    outgoing = placed.astype(jnp.bfloat16).reshape(owners, local_experts * capacity, width_here)
    arrived = lax.all_to_all(outgoing, "dp", split_axis=0, concat_axis=0, tiled=True)
    rows = lax.all_gather(arrived, "tensor", axis=2, tiled=True).reshape(
        owners, local_experts, capacity, model_width
    )
    ff_here = down_weight.shape[1]
    down_split = down_weight.reshape(local_experts, ff_here, tensor_size, width_here).transpose(
        2, 0, 1, 3
    )
    half_experts = local_experts // 2
    down_first = lax.all_to_all(down_split[:, :half_experts], "tensor", 0, 0, tiled=True)
    rows, down_first = lax.optimization_barrier((rows, down_first))
    gate_val = jnp.einsum("necd,edf->necf", rows, gate_weight, preferred_element_type=jnp.float32)
    lift_val = jnp.einsum("necd,edf->necf", rows, lift_weight, preferred_element_type=jnp.float32)
    hidden_units = (jax.nn.silu(gate_val) * lift_val).astype(jnp.bfloat16)
    hidden_all = lax.all_gather(hidden_units, "tensor", axis=0)
    down_second = lax.all_to_all(down_split[:, half_experts:], "tensor", 0, 0, tiled=True)
    down_cols = jnp.concatenate([down_first, down_second], axis=1)
    summed_out = jnp.einsum(
        "tnecf,tefd->necd", hidden_all, down_cols, preferred_element_type=jnp.float32
    ).astype(jnp.bfloat16)
    returned = lax.all_to_all(
        summed_out.reshape(owners, local_experts * capacity, width_here),
        "dp",
        split_axis=0,
        concat_axis=0,
        tiled=True,
    ).astype(jnp.float32)
    returned = returned.reshape(experts_all * capacity, width_here)
    picked_rows = returned[code_of]
    moe_cols = jnp.sum(share[:, :, None] * picked_rows, axis=1).astype(jnp.bfloat16)
    moe_out = lax.all_to_all(moe_cols, "tensor", split_axis=0, concat_axis=1, tiled=True)
    layer_out = (middle.astype(jnp.float32) + moe_out.astype(jnp.float32)).astype(jnp.bfloat16)
    return (layer_out, new_rows)


def solution(mesh):
    in_specs = (
        P(("dp", "tensor"), None),
        P(),
        P(None, "tensor"),
        P(None, "tensor"),
        P(),
        P(),
        P("tensor", None),
        P(),
        P("dp", None, "tensor"),
        P("dp", None, "tensor"),
        P("dp", "tensor", None),
        P("dp", None),
        P("dp", None),
        P("dp", "tensor", None),
        P("dp", "tensor", None),
        P("dp"),
        P("dp"),
        P("dp"),
    )
    out_specs = (P(("dp", "tensor"), None), P("dp", "tensor"))
    return jax.shard_map(body, mesh=mesh, in_specs=in_specs, out_specs=out_specs, check_vma=False)
```

```python
import math

import jax
import jax.numpy as jnp
from jax import lax
from jax.sharding import PartitionSpec as P

EPSILON = 1e-06
THETA = 1000000.0
NEGATIVE = -1e30


def rms_scale(values, gain):
    mean_square = jnp.mean(values * values, axis=-1, keepdims=True)
    return values * lax.rsqrt(mean_square + EPSILON) * gain


def rotate(values, positions):
    half = values.shape[-1] // 2
    freqs = THETA ** (-jnp.arange(half).astype(jnp.float32) * 2.0 / values.shape[-1])
    angles = positions.astype(jnp.float32)[:, None] * freqs[None, :]
    angles = jnp.concatenate([angles, angles], axis=-1)
    cosine = jnp.cos(angles)[:, None, :]
    sine = jnp.sin(angles)[:, None, :]
    turned = jnp.concatenate([-values[..., half:], values[..., :half]], axis=-1)
    return values * cosine + turned * sine


def body(
    residual_in,
    attn_gain,
    query_weight,
    kv_weight,
    query_gain,
    key_gain,
    out_weight,
    moe_gain,
    gate_weight,
    lift_weight,
    down_weight,
    routes,
    route_weights,
    prefix_cache,
    suffix_cache,
    prefix_len,
    suffix_len,
    request_group,
):
    tensor_size = lax.axis_size("tensor")
    tensor_rank = lax.axis_index("tensor")
    dp_rank = lax.axis_index("dp")
    owners = lax.axis_size("dp")
    head_dim = query_gain.shape[0]
    requests = routes.shape[0]
    model_width = residual_in.shape[1]
    query_cols = query_weight.shape[1]
    kv_cols = kv_weight.shape[1]
    heads_here = query_cols // head_dim
    heads_all = heads_here * tensor_size
    kv_heads_all = kv_cols * tensor_size // (2 * head_dim)
    per_group = heads_all // kv_heads_all
    groups_dev = prefix_cache.shape[0]
    pre_local = prefix_cache.shape[1]
    suf_local = suffix_cache.shape[1]
    residual_all = lax.all_to_all(
        jnp.broadcast_to(residual_in[None], (tensor_size,) + residual_in.shape),
        "tensor",
        0,
        0,
        tiled=True,
    ).reshape(-1, residual_in.shape[1])
    piece = rms_scale(residual_all.astype(jnp.float32), attn_gain).astype(jnp.bfloat16)
    projected = jnp.concatenate(
        [
            jnp.dot(piece, query_weight, preferred_element_type=jnp.float32),
            jnp.dot(piece, kv_weight, preferred_element_type=jnp.float32),
        ],
        axis=1,
    )
    query_raw = projected[:, :query_cols].reshape(requests, heads_here, head_dim)
    kv_raw = projected[:, query_cols:].reshape(requests, kv_cols // head_dim, head_dim)
    group_ids = dp_rank * groups_dev + jnp.arange(groups_dev)
    member = request_group[:, None] == group_ids[None, :]
    prefix_of = jnp.sum(jnp.where(member, prefix_len[None, :], 0), axis=1)
    positions = prefix_of + suffix_len
    queries = rotate(rms_scale(query_raw, query_gain), positions).astype(jnp.bfloat16)
    head_number = tensor_rank * (kv_cols // head_dim) + jnp.arange(kv_cols // head_dim)
    is_key = (head_number < kv_heads_all)[None, :, None]
    keyed = rotate(rms_scale(kv_raw, key_gain), positions)
    new_rows = jnp.where(is_key, keyed, kv_raw).astype(jnp.bfloat16).reshape(requests, kv_cols)
    joined = jnp.concatenate([queries.reshape(requests, query_cols), new_rows], axis=1)
    every_head = lax.all_to_all(
        jnp.broadcast_to(joined[None], (tensor_size,) + joined.shape), "tensor", 0, 0, tiled=True
    ).transpose(1, 0, 2)
    all_queries = every_head[:, :, :query_cols].reshape(requests, kv_heads_all, per_group, head_dim)
    all_kv = every_head[:, :, query_cols:]
    own_keys = all_kv[:, :kv_heads_all]
    own_values = all_kv[:, kv_heads_all:].astype(jnp.float32)
    scale = 1.0 / math.sqrt(head_dim)
    split_at = kv_heads_all * head_dim
    pre_keys = prefix_cache[:, :, :split_at].reshape(groups_dev, pre_local, kv_heads_all, head_dim)
    pre_values = prefix_cache[:, :, split_at:].reshape(
        groups_dev, pre_local, kv_heads_all, head_dim
    )
    suf_keys = suffix_cache[:, :, :split_at].reshape(requests, suf_local, kv_heads_all, head_dim)
    suf_values = suffix_cache[:, :, split_at:].reshape(requests, suf_local, kv_heads_all, head_dim)
    pre_scores = (
        jnp.einsum("rgqd,npgd->rgqnp", all_queries, pre_keys, preferred_element_type=jnp.float32)
        * scale
    )
    suf_scores = (
        jnp.einsum("rgqd,rsgd->rgqs", all_queries, suf_keys, preferred_element_type=jnp.float32)
        * scale
    )
    own_scores = (
        jnp.einsum("rgqd,rgd->rgq", all_queries, own_keys, preferred_element_type=jnp.float32)
        * scale
    )
    pre_slots = tensor_rank * pre_local + jnp.arange(pre_local)
    pre_valid = (member[:, :, None] & (pre_slots[None, None, :] < prefix_len[None, :, None]))[
        :, None, None, :, :
    ]
    suf_slots = tensor_rank * suf_local + jnp.arange(suf_local)
    suf_valid = (suf_slots[None, :] < suffix_len[:, None])[:, None, None, :]
    own_valid = tensor_rank == 0
    top_pre = jnp.max(jnp.where(pre_valid, pre_scores, NEGATIVE), axis=(3, 4))
    top_suf = jnp.max(jnp.where(suf_valid, suf_scores, NEGATIVE), axis=3)
    top_own = jnp.where(own_valid, own_scores, NEGATIVE)
    top_local = (
        jnp.maximum(jnp.maximum(top_pre, top_suf), top_own).astype(jnp.bfloat16).astype(jnp.float32)
    )
    pre_weights = jnp.where(pre_valid, jnp.exp(pre_scores - top_local[..., None, None]), 0.0)
    suf_weights = jnp.where(suf_valid, jnp.exp(suf_scores - top_local[..., None]), 0.0)
    own_weights = jnp.where(own_valid, jnp.exp(own_scores - top_local), 0.0)
    total_local = jnp.sum(pre_weights, axis=(3, 4)) + jnp.sum(suf_weights, axis=3) + own_weights
    sums_local = jnp.einsum(
        "rgqnp,npgd->rgqd",
        pre_weights.astype(jnp.bfloat16),
        pre_values,
        preferred_element_type=jnp.float32,
    )
    sums_local = sums_local + jnp.einsum(
        "rgqs,rsgd->rgqd",
        suf_weights.astype(jnp.bfloat16),
        suf_values,
        preferred_element_type=jnp.float32,
    )
    own_low = own_weights.astype(jnp.bfloat16).astype(jnp.float32)
    sums_local = sums_local + own_low[..., None] * own_values[:, :, None, :]
    pair_rows = requests * heads_here // head_dim

    def by_owner(values):
        values = values.reshape(requests, tensor_size, heads_here, -1).transpose(1, 0, 2, 3)
        return values.reshape(tensor_size, -1, head_dim)

    total_high = total_local.astype(jnp.bfloat16)
    total_low = (total_local - total_high.astype(jnp.float32)).astype(jnp.bfloat16)
    packed = jnp.concatenate(
        [
            by_owner(sums_local.astype(jnp.bfloat16)),
            by_owner(top_local.astype(jnp.bfloat16)),
            by_owner(total_high),
            by_owner(total_low),
        ],
        axis=1,
    )
    parts = lax.all_to_all(packed, "tensor", 0, 0, tiled=True).astype(jnp.float32)
    spread = requests * heads_here
    part_sums = parts[:, :spread].reshape(tensor_size, requests, heads_here, head_dim)
    part_top = parts[:, spread : spread + pair_rows].reshape(tensor_size, requests, heads_here)
    part_total = (
        parts[:, spread + pair_rows : spread + 2 * pair_rows]
        + parts[:, spread + 2 * pair_rows :]
    ).reshape(tensor_size, requests, heads_here)
    top_all = jnp.max(part_top, axis=0)
    factor = jnp.exp(part_top - top_all[None])
    total_mine = jnp.sum(part_total * factor, axis=0)
    sums_mine = jnp.sum(part_sums * factor[..., None], axis=0)
    mixed = sums_mine / total_mine[..., None]
    attn_heads = mixed.reshape(requests, query_cols).astype(jnp.bfloat16)
    width_here = model_width // tensor_size
    tokens_here = residual_in.shape[0]
    attn_parts = lax.all_to_all(
        jnp.dot(attn_heads, out_weight, preferred_element_type=jnp.float32).astype(jnp.bfloat16),
        "tensor",
        split_axis=0,
        concat_axis=0,
        tiled=True,
    ).reshape(tensor_size, tokens_here, model_width)
    attn_out = jnp.sum(attn_parts.astype(jnp.float32), axis=0)
    middle = (residual_in.astype(jnp.float32) + attn_out).astype(jnp.bfloat16)
    moe_in = rms_scale(middle.astype(jnp.float32), moe_gain).astype(jnp.bfloat16)
    cols_in = lax.all_to_all(moe_in, "tensor", split_axis=1, concat_axis=0, tiled=True)
    local_experts = gate_weight.shape[0]
    experts_all = local_experts * owners
    topk = routes.shape[1]
    capacity = 2 * requests * topk // experts_all
    flat_routes = routes.reshape(-1)
    onehot = (flat_routes[:, None] == jnp.arange(experts_all)[None, :]).astype(jnp.int32)
    running = jnp.cumsum(onehot, axis=0)
    slot_of = jnp.sum(onehot * running, axis=1) - 1
    code_of = (flat_routes * capacity + slot_of).reshape(requests, topk)
    code_span = jnp.arange(experts_all * capacity)
    placing = jnp.any(code_of[None, :, :] == code_span[:, None, None], axis=2).astype(jnp.bfloat16)
    share = route_weights / jnp.sum(route_weights, axis=1, keepdims=True)
    placed = jnp.dot(placing, cols_in, preferred_element_type=jnp.float32)
    outgoing = placed.astype(jnp.bfloat16).reshape(owners, local_experts * capacity, width_here)
    arrived = lax.all_to_all(outgoing, "dp", split_axis=0, concat_axis=0, tiled=True)
    rows = lax.all_gather(arrived, "tensor", axis=2, tiled=True).reshape(
        owners, local_experts, capacity, model_width
    )
    ff_here = down_weight.shape[1]
    down_split = down_weight.reshape(local_experts, ff_here, tensor_size, width_here).transpose(
        2, 0, 1, 3
    )
    half_experts = 3 * local_experts // 4
    down_first = lax.all_to_all(down_split[:, :half_experts], "tensor", 0, 0, tiled=True)
    rows, down_first = lax.optimization_barrier((rows, down_first))
    gate_val = jnp.einsum("necd,edf->necf", rows, gate_weight, preferred_element_type=jnp.float32)
    lift_val = jnp.einsum("necd,edf->necf", rows, lift_weight, preferred_element_type=jnp.float32)
    hidden_units = (jax.nn.silu(gate_val) * lift_val).astype(jnp.bfloat16)
    hidden_all = lax.all_gather(hidden_units, "tensor", axis=0)
    down_second = lax.all_to_all(down_split[:, half_experts:], "tensor", 0, 0, tiled=True)
    down_cols = jnp.concatenate([down_first, down_second], axis=1)
    summed_out = jnp.einsum(
        "tnecf,tefd->necd", hidden_all, down_cols, preferred_element_type=jnp.float32
    ).astype(jnp.bfloat16)
    returned = lax.all_to_all(
        summed_out.reshape(owners, local_experts * capacity, width_here),
        "dp",
        split_axis=0,
        concat_axis=0,
        tiled=True,
    ).astype(jnp.float32)
    returned = returned.reshape(experts_all * capacity, width_here)
    picked_rows = returned[code_of]
    moe_cols = jnp.sum(share[:, :, None] * picked_rows, axis=1).astype(jnp.bfloat16)
    moe_out = lax.all_to_all(moe_cols, "tensor", split_axis=0, concat_axis=1, tiled=True)
    layer_out = (middle.astype(jnp.float32) + moe_out.astype(jnp.float32)).astype(jnp.bfloat16)
    return (layer_out, new_rows)


def solution(mesh):
    in_specs = (
        P(("dp", "tensor"), None),
        P(),
        P(None, "tensor"),
        P(None, "tensor"),
        P(),
        P(),
        P("tensor", None),
        P(),
        P("dp", None, "tensor"),
        P("dp", None, "tensor"),
        P("dp", "tensor", None),
        P("dp", None),
        P("dp", None),
        P("dp", "tensor", None),
        P("dp", "tensor", None),
        P("dp"),
        P("dp"),
        P("dp"),
    )
    out_specs = (P(("dp", "tensor"), None), P("dp", "tensor"))
    return jax.shard_map(body, mesh=mesh, in_specs=in_specs, out_specs=out_specs, check_vma=False)
```
